256 devices in a mesh: ctx: 64 (over y, z, core), ch: 4 (over x).
Axes of the slice: x: 4, y: 4, z: 8, core: 2. Of those that a mesh axis runs over, the one named last changes fastest.
Arguments:
- tokens: bfloat16 [16384, 4096], P('ctx', 'ch'), may hold values from -6 to 6
- in_weight: bfloat16 [3, 4096, 4096], P(None, 'ctx', 'ch'), may hold values from -0.09375 to 0.09375
- short_taps: float32 [3, 3, 4096], P(None, None, 'ch'), may hold values from -4 to 4
- long_filter: float32 [4, 1024, 16384], P('ch', 'ctx'), may hold values from -0.046875 to 0.046875
- skip_gain: float32 [4, 1024], P('ch', 'ctx'), may hold values from 0.25 to 2
Outputs:
- gated_output: bfloat16 [4096, 16384], P('ch', 'ctx')
The draws below stay inside these ranges and needn't reach their ends.
All inputs are finite; a program needn't handle non-finite values.
Results may differ from the reference program's by a relative error of at most 0.015.
Values may be sent and summed in bfloat16 or wider, within the bound.
No kernel may reach another device: no remote copies, remote signals or barrier semaphores. Data moves between devices by JAX's collectives and lax.ppermute only.
A program may use at most 128 MiB of HBM per device.

```python
import math
import jax
import jax.numpy as jnp
from jax import lax

D = 4096
LANE_TOTAL = 4096
SITE_SPAN = 16384
N_CH = 4


def block_levels(own_key, shape, split, least, high):
    factor_of = 1.0
    for dim, blocks in split:
        draws = jax.random.uniform(jax.random.fold_in(jax.random.fold_in(own_key, 6), dim), (blocks,), jnp.float32, least / len(split), high / len(split))
        factor_of = factor_of * jnp.repeat(jnp.exp(draws), shape[dim] // blocks).reshape((-1,) + (1,) * (len(shape) - 1 - dim))
    return factor_of


def bell_draw(rng, shape, width, reach, shards=(), dtype=jnp.bfloat16):
    values = jax.random.normal(rng, shape, jnp.float32) * width
    if len(shards) > 0:
        values = block_levels(rng, shape, shards, -0.22, 0.18) * values
    return jnp.clip(values, min=-reach, max=reach).astype(dtype)


def setup_inputs(seed: int = 0) -> dict:
    key_of = jax.random.split(jax.random.key(seed), 6)
    return {
        "tokens": bell_draw(key_of[0], (SITE_SPAN, D), 1.0, 6.0, ((0, 64), (1, 4))),
        "in_weight": bell_draw(key_of[1], (3, D, LANE_TOTAL), D ** -0.5, 0.09375, ((1, 64), (2, 4))),
        "short_taps": bell_draw(key_of[2], (3, 3, LANE_TOTAL), 0.6, 4.0, ((2, 4),), jnp.float32),
        "long_filter": bell_draw(key_of[3], (N_CH, LANE_TOTAL // N_CH, SITE_SPAN), SITE_SPAN ** -0.5, 0.046875, ((0, 4), (1, 64)), jnp.float32),
        "skip_gain": jnp.clip(jnp.exp(math.log(2.0) - 2.0794415 * jax.random.uniform(key_of[4], (N_CH, LANE_TOTAL // N_CH), jnp.float32) ** block_levels(key_of[4], (N_CH, LANE_TOTAL // N_CH), ((0, 4), (1, 64)), -0.2, 0.2)), 0.25, 2.0),
    }


def short_conv(projected_float, short_taps):
    context_extent = projected_float.shape[2]
    padded = jnp.pad(projected_float, ((0, 0), (0, 0), (2, 0)))
    result = jnp.zeros_like(projected_float)
    for offset in range(3):
        result = result + short_taps[:, offset, :][:, :, None] * padded[:, :, 2 - offset:2 - offset + context_extent]
    return result


def reference(tokens, in_weight, short_taps, long_filter, skip_gain):
    projected = jnp.stack([jnp.dot(in_weight[which_panel].T, tokens.T, preferred_element_type=jnp.float32) for which_panel in range(3)]).astype(jnp.bfloat16)
    embedding_result = short_conv(projected.astype(jnp.float32), short_taps)
    gate_wave = (embedding_result[1] * embedding_result[2]).astype(jnp.bfloat16)
    kernel_collection = long_filter.reshape(LANE_TOTAL, SITE_SPAN)
    leftover_lines = skip_gain.reshape(LANE_TOTAL)
    lines_in_tile = min(LANE_TOTAL, 256)

    def causal_smear(tile_fragments):
        gate_wave_lines, kernel_table_lines, leftover_fragment = tile_fragments
        padded_extent = 2 * SITE_SPAN
        gate_wave_wide = gate_wave_lines.astype(jnp.float32)
        fourier_coefficients = jnp.fft.rfft(gate_wave_wide, n=padded_extent) * jnp.fft.rfft(kernel_table_lines, n=padded_extent)
        affine_mapping = jnp.fft.irfft(fourier_coefficients, n=padded_extent)[:, :SITE_SPAN]
        return (affine_mapping + leftover_fragment[:, None] * gate_wave_wide).astype(jnp.bfloat16)

    blended_lines = lax.map(causal_smear, (gate_wave.reshape(LANE_TOTAL // lines_in_tile, lines_in_tile, SITE_SPAN), kernel_collection.reshape(LANE_TOTAL // lines_in_tile, lines_in_tile, SITE_SPAN), leftover_lines.reshape(LANE_TOTAL // lines_in_tile, lines_in_tile))).reshape(LANE_TOTAL, SITE_SPAN)
    gated_output = (embedding_result[0] * blended_lines.astype(jnp.float32)).astype(jnp.bfloat16)
    return gated_output
```

```python
import math

import jax
import jax.numpy as jnp
import numpy as np
from jax import lax
from jax.sharding import Mesh, NamedSharding
from jax.sharding import PartitionSpec as P

BLOCK = 1024
FACTOR = 32
CTX = ("cc", "cr")


def shifted(block, axis, size, distance):
    route = [(i - distance, i) for i in range(size) if 0 <= i - distance < size]
    return lax.ppermute(block, axis, route)


def unit_wave(rows, cols, period, scale_rows):
    outer = rows // FACTOR
    hi = jnp.arange(outer, dtype=jnp.int32)[:, None] * (FACTOR * scale_rows)
    lo = jnp.arange(FACTOR, dtype=jnp.int32)[:, None] * scale_rows
    col = jnp.arange(cols, dtype=jnp.int32)[None, :]
    step = 2.0 * math.pi / period
    hi_phase = step * ((hi * col) % period).astype(jnp.float32)
    lo_phase = step * ((lo * col) % period).astype(jnp.float32)
    hc, hs = jnp.cos(hi_phase)[:, None, :], jnp.sin(hi_phase)[:, None, :]
    lc, ls = jnp.cos(lo_phase)[None, :, :], jnp.sin(lo_phase)[None, :, :]
    cos_t = (hc * lc - hs * ls).reshape(rows, cols)
    sin_t = (hs * lc + hc * ls).reshape(rows, cols)
    return cos_t, sin_t


def spectral_tables(tile_extent):
    period = 2 * tile_extent
    cos_f, sin_f = unit_wave(tile_extent, tile_extent, period, 1)
    alternating = jnp.where(jnp.arange(tile_extent) % 2 == 0, 1.0, -1.0).astype(jnp.float32)
    first_col = (jnp.arange(tile_extent) == 0)[None, :]
    forward = jnp.concatenate(
        [cos_f, jnp.where(first_col, alternating[:, None], -sin_f)], axis=1
    ).astype(jnp.bfloat16)
    cos_b, sin_b = unit_wave(tile_extent, period, period, 1)
    first_row = (jnp.arange(tile_extent) == 0)[:, None]
    alt_t = jnp.where(jnp.arange(period) % 2 == 0, 1.0, -1.0).astype(jnp.float32)[None, :]
    weights = jnp.where(first_row, 1.0, 2.0) / period
    inverse = jnp.concatenate(
        [weights * cos_b, jnp.where(first_row, alt_t / period, -(2.0 / period) * sin_b)], axis=0
    ).astype(jnp.bfloat16)
    return forward, inverse


def global_causal_smear(gate_wave, kernel_table_lines, leftover_lines, tile_extent):
    lane_total, context_extent = gate_wave.shape
    groups = context_extent // tile_extent
    forward, inverse = spectral_tables(tile_extent)
    slot0 = (jnp.arange(tile_extent) == 0)[None, None, :]
    source = gate_wave.reshape(lane_total * groups, tile_extent)
    kernel = kernel_table_lines.astype(jnp.bfloat16).reshape(lane_total * groups, tile_extent)
    spec_x = jnp.dot(source, forward, preferred_element_type=jnp.float32)
    spec_k = jnp.dot(kernel, forward, preferred_element_type=jnp.float32)
    spec_x = spec_x.reshape(lane_total, groups, 2 * tile_extent)
    spec_k = spec_k.reshape(lane_total, groups, 2 * tile_extent)
    x_re, x_im = spec_x[:, :, :tile_extent], spec_x[:, :, tile_extent:]
    k_re, k_im = spec_k[:, :, :tile_extent], spec_k[:, :, tile_extent:]
    pad = jnp.zeros((lane_total, groups - 1, tile_extent), jnp.float32)
    xp_re = jnp.concatenate([pad, x_re], axis=1)
    xp_im = jnp.concatenate([pad, x_im], axis=1)
    rr = ii = ri = ir = None
    for offset in range(groups):
        s_re = xp_re[:, groups - 1 - offset : 2 * groups - 1 - offset]
        s_im = xp_im[:, groups - 1 - offset : 2 * groups - 1 - offset]
        f_re = k_re[:, offset : offset + 1]
        f_im = k_im[:, offset : offset + 1]
        terms = (f_re * s_re, f_im * s_im, f_re * s_im, f_im * s_re)
        if rr is None:
            rr, ii, ri, ir = terms
        else:
            rr, ii, ri, ir = rr + terms[0], ii + terms[1], ri + terms[2], ir + terms[3]
    y_re = rr - jnp.where(slot0, 0.0, ii)
    y_im = jnp.where(slot0, ii, ri + ir)
    packed = jnp.concatenate([y_re, y_im], axis=2).astype(jnp.bfloat16)
    rows = jnp.dot(
        packed.reshape(lane_total * groups, 2 * tile_extent),
        inverse,
        preferred_element_type=jnp.float32,
    ).reshape(lane_total, groups, 2 * tile_extent)
    front_half = rows[:, :, :tile_extent]
    back_half = rows[:, :, tile_extent:]
    carried = jnp.concatenate(
        [jnp.zeros((lane_total, 1, tile_extent), jnp.float32), back_half[:, :-1]], axis=1
    )
    affine_mapping = (front_half + carried).reshape(lane_total, context_extent)
    wide = gate_wave.astype(jnp.float32)
    return (affine_mapping + leftover_lines[:, None] * wide).astype(jnp.bfloat16)


def short_conv(projected_float, local_taps, previous):
    context_extent = projected_float.shape[2]
    extended = jnp.concatenate([previous, projected_float], axis=2)
    result = jnp.zeros_like(projected_float)
    for offset in range(3):
        result = (
            result
            + local_taps[:, offset, :][:, :, None]
            * extended[:, :, 2 - offset : 2 - offset + context_extent]
        )
    return result


def make_shards(n_ctx, tile_extent):
    def project(weight_local, both_tokens):
        halves = lax.all_to_all(weight_local, "cr", split_axis=2, concat_axis=1, tiled=True)
        whole = lax.all_gather(halves, "cc", axis=1, tiled=True)
        summed = jnp.einsum("pdc,ld->pcl", whole, both_tokens, preferred_element_type=jnp.float32)
        mine = summed.astype(jnp.bfloat16)
        return lax.all_to_all(mine, "cr", split_axis=2, concat_axis=1, tiled=True)

    def featured(projected, taps):
        local_tokens = projected.shape[2]
        previous = shifted(projected[:, :, local_tokens - 2 :], CTX, n_ctx, 1)
        return short_conv(projected.astype(jnp.float32), taps, previous.astype(jnp.float32))

    def shards(tokens, in_weight, short_taps, long_filter, skip_gain):
        row_tokens = lax.all_gather(tokens, "ch", axis=1, tiled=True)
        both_tokens = lax.all_gather(row_tokens, "cr", axis=0, tiled=True)
        projected12 = project(in_weight[1:3], both_tokens)
        embed12 = featured(projected12, short_taps[1:3])
        gate_wave = (embed12[0] * embed12[1]).astype(jnp.bfloat16)
        weight0, gate_wave = lax.optimization_barrier((in_weight[0:1], gate_wave))
        per_channel_view = lax.all_to_all(gate_wave, CTX, split_axis=0, concat_axis=1, tiled=True)
        blended_lines = global_causal_smear(
            per_channel_view, long_filter[0], skip_gain[0], tile_extent
        )
        projected0 = project(weight0, both_tokens)
        embed0 = featured(projected0, short_taps[0:1])
        by_token = lax.all_to_all(blended_lines, CTX, split_axis=1, concat_axis=0, tiled=True)
        gated_output = (embed0[0] * by_token.astype(jnp.float32)).astype(jnp.bfloat16)
        return gated_output

    return shards


def solution(mesh):
    n_ctx = mesh.shape["ctx"]
    grid = np.asarray(mesh.devices).reshape(n_ctx // 2, 2, mesh.shape["ch"])
    split_mesh = Mesh(grid, ("cc", "cr", "ch"))
    placed = (
        P(CTX, "ch"),
        P(None, CTX, "ch"),
        P(None, None, "ch"),
        P("ch", CTX, None),
        P("ch", CTX),
    )
    mapped = jax.shard_map(
        make_shards(n_ctx, BLOCK),
        mesh=split_mesh,
        in_specs=placed,
        out_specs=P("ch", CTX),
        check_vma=False,
    )
    out_sharding = NamedSharding(mesh, P("ch", "ctx"))

    def run(*args):
        return lax.with_sharding_constraint(mapped(*args), out_sharding)

    return run
```

```python
import math

import jax
import jax.numpy as jnp
from jax import lax
from jax.sharding import PartitionSpec as P

BLOCK = 1024
FACTOR = 32


def shifted(block, axis, size, distance):
    route = [(i - distance, i) for i in range(size) if 0 <= i - distance < size]
    return lax.ppermute(block, axis, route)


def unit_wave(rows, cols, period, scale_rows):
    outer = rows // FACTOR
    hi = jnp.arange(outer, dtype=jnp.int32)[:, None] * (FACTOR * scale_rows)
    lo = jnp.arange(FACTOR, dtype=jnp.int32)[:, None] * scale_rows
    col = jnp.arange(cols, dtype=jnp.int32)[None, :]
    step = 2.0 * math.pi / period
    hi_phase = step * ((hi * col) % period).astype(jnp.float32)
    lo_phase = step * ((lo * col) % period).astype(jnp.float32)
    hc, hs = jnp.cos(hi_phase)[:, None, :], jnp.sin(hi_phase)[:, None, :]
    lc, ls = jnp.cos(lo_phase)[None, :, :], jnp.sin(lo_phase)[None, :, :]
    cos_t = (hc * lc - hs * ls).reshape(rows, cols)
    sin_t = (hs * lc + hc * ls).reshape(rows, cols)
    return cos_t, sin_t


def spectral_tables(tile_extent):
    period = 2 * tile_extent
    cos_f, sin_f = unit_wave(tile_extent, tile_extent, period, 1)
    alternating = jnp.where(jnp.arange(tile_extent) % 2 == 0, 1.0, -1.0).astype(jnp.float32)
    first_col = (jnp.arange(tile_extent) == 0)[None, :]
    forward = jnp.concatenate(
        [cos_f, jnp.where(first_col, alternating[:, None], -sin_f)], axis=1
    ).astype(jnp.bfloat16)
    cos_b, sin_b = unit_wave(tile_extent, period, period, 1)
    first_row = (jnp.arange(tile_extent) == 0)[:, None]
    alt_t = jnp.where(jnp.arange(period) % 2 == 0, 1.0, -1.0).astype(jnp.float32)[None, :]
    weights = jnp.where(first_row, 1.0, 2.0) / period
    inverse = jnp.concatenate(
        [weights * cos_b, jnp.where(first_row, alt_t / period, -(2.0 / period) * sin_b)], axis=0
    ).astype(jnp.bfloat16)
    return forward, inverse


def global_causal_smear(gate_wave, kernel_table_lines, leftover_lines, tile_extent):
    lane_total, context_extent = gate_wave.shape
    groups = context_extent // tile_extent
    forward, inverse = spectral_tables(tile_extent)
    slot0 = (jnp.arange(tile_extent) == 0)[None, None, :]
    source = gate_wave.reshape(lane_total * groups, tile_extent)
    kernel = kernel_table_lines.astype(jnp.bfloat16).reshape(lane_total * groups, tile_extent)
    spec_x = jnp.dot(source, forward, preferred_element_type=jnp.float32)
    spec_k = jnp.dot(kernel, forward, preferred_element_type=jnp.float32)
    spec_x = spec_x.reshape(lane_total, groups, 2 * tile_extent)
    spec_k = spec_k.reshape(lane_total, groups, 2 * tile_extent)
    x_re, x_im = spec_x[:, :, :tile_extent], spec_x[:, :, tile_extent:]
    k_re, k_im = spec_k[:, :, :tile_extent], spec_k[:, :, tile_extent:]
    pad = jnp.zeros((lane_total, groups - 1, tile_extent), jnp.float32)
    xp_re = jnp.concatenate([pad, x_re], axis=1)
    xp_im = jnp.concatenate([pad, x_im], axis=1)
    rr = ii = ri = ir = None
    for offset in range(groups):
        s_re = xp_re[:, groups - 1 - offset : 2 * groups - 1 - offset]
        s_im = xp_im[:, groups - 1 - offset : 2 * groups - 1 - offset]
        f_re = k_re[:, offset : offset + 1]
        f_im = k_im[:, offset : offset + 1]
        terms = (f_re * s_re, f_im * s_im, f_re * s_im, f_im * s_re)
        if rr is None:
            rr, ii, ri, ir = terms
        else:
            rr, ii, ri, ir = rr + terms[0], ii + terms[1], ri + terms[2], ir + terms[3]
    y_re = rr - jnp.where(slot0, 0.0, ii)
    y_im = jnp.where(slot0, ii, ri + ir)
    packed = jnp.concatenate([y_re, y_im], axis=2).astype(jnp.bfloat16)
    rows = jnp.dot(
        packed.reshape(lane_total * groups, 2 * tile_extent),
        inverse,
        preferred_element_type=jnp.float32,
    ).reshape(lane_total, groups, 2 * tile_extent)
    front_half = rows[:, :, :tile_extent]
    back_half = rows[:, :, tile_extent:]
    carried = jnp.concatenate(
        [jnp.zeros((lane_total, 1, tile_extent), jnp.float32), back_half[:, :-1]], axis=1
    )
    affine_mapping = (front_half + carried).reshape(lane_total, context_extent)
    wide = gate_wave.astype(jnp.float32)
    return (affine_mapping + leftover_lines[:, None] * wide).astype(jnp.bfloat16)


def short_conv(projected_float, local_taps, previous):
    context_extent = projected_float.shape[2]
    extended = jnp.concatenate([previous, projected_float], axis=2)
    result = jnp.zeros_like(projected_float)
    for offset in range(3):
        result = (
            result
            + local_taps[:, offset, :][:, :, None]
            * extended[:, :, 2 - offset : 2 - offset + context_extent]
        )
    return result


def make_shards(n_ctx, n_ch, tile_extent):
    def project(weight_local, whole_tokens):
        whole = lax.all_gather(weight_local, "ctx", axis=1, tiled=True)
        summed = jnp.einsum("pdc,ld->pcl", whole, whole_tokens, preferred_element_type=jnp.float32)
        return summed.astype(jnp.bfloat16)

    def featured(projected, taps):
        local_tokens = projected.shape[2]
        previous = shifted(projected[:, :, local_tokens - 2 :], "ctx", n_ctx, 1)
        return short_conv(projected.astype(jnp.float32), taps, previous.astype(jnp.float32))

    def shards(tokens, in_weight, short_taps, long_filter, skip_gain):
        local_tokens, local_features = tokens.shape
        copies = jnp.broadcast_to(tokens[None], (n_ch, local_tokens, local_features))
        pieces = lax.all_to_all(copies, "ch", split_axis=0, concat_axis=0, tiled=True)
        whole_tokens = pieces.transpose(1, 0, 2).reshape(local_tokens, n_ch * local_features)
        projected12 = project(in_weight[1:3], whole_tokens)
        embed12 = featured(projected12, short_taps[1:3])
        gate_wave = (embed12[0] * embed12[1]).astype(jnp.bfloat16)
        weight0, gate_wave = lax.optimization_barrier((in_weight[0:1], gate_wave))
        per_channel_view = lax.all_to_all(gate_wave, "ctx", split_axis=0, concat_axis=1, tiled=True)
        blended_lines = global_causal_smear(
            per_channel_view, long_filter[0], skip_gain[0], tile_extent
        )
        projected0 = project(weight0, whole_tokens)
        embed0 = featured(projected0, short_taps[0:1])
        by_token = lax.all_to_all(blended_lines, "ctx", split_axis=1, concat_axis=0, tiled=True)
        gated_output = (embed0[0] * by_token.astype(jnp.float32)).astype(jnp.bfloat16)
        return gated_output

    return shards


def solution(mesh):
    placed = (
        P("ctx", "ch"),
        P(None, "ctx", "ch"),
        P(None, None, "ch"),
        P("ch", "ctx", None),
        P("ch", "ctx"),
    )
    return jax.shard_map(
        make_shards(mesh.shape["ctx"], mesh.shape["ch"], BLOCK),
        mesh=mesh,
        in_specs=placed,
        out_specs=P("ch", "ctx"),
        check_vma=False,
    )
```

```python
import math

import jax
import jax.numpy as jnp
from jax import lax
from jax.sharding import PartitionSpec as P

BLOCK = 1024
FACTOR = 32


def shifted(block, axis, size, distance):
    route = [(i - distance, i) for i in range(size) if 0 <= i - distance < size]
    return lax.ppermute(block, axis, route)


def unit_wave(rows, cols, period, scale_rows):
    outer = rows // FACTOR
    hi = jnp.arange(outer, dtype=jnp.int32)[:, None] * (FACTOR * scale_rows)
    lo = jnp.arange(FACTOR, dtype=jnp.int32)[:, None] * scale_rows
    col = jnp.arange(cols, dtype=jnp.int32)[None, :]
    step = 2.0 * math.pi / period
    hi_phase = step * ((hi * col) % period).astype(jnp.float32)
    lo_phase = step * ((lo * col) % period).astype(jnp.float32)
    hc, hs = jnp.cos(hi_phase)[:, None, :], jnp.sin(hi_phase)[:, None, :]
    lc, ls = jnp.cos(lo_phase)[None, :, :], jnp.sin(lo_phase)[None, :, :]
    cos_t = (hc * lc - hs * ls).reshape(rows, cols)
    sin_t = (hs * lc + hc * ls).reshape(rows, cols)
    return cos_t, sin_t


def spectral_tables(tile_extent):
    period = 2 * tile_extent
    cos_f, sin_f = unit_wave(tile_extent, tile_extent, period, 1)
    alternating = jnp.where(jnp.arange(tile_extent) % 2 == 0, 1.0, -1.0).astype(jnp.float32)
    first_col = (jnp.arange(tile_extent) == 0)[None, :]
    forward = jnp.concatenate(
        [cos_f, jnp.where(first_col, alternating[:, None], -sin_f)], axis=1
    ).astype(jnp.bfloat16)
    cos_b, sin_b = unit_wave(tile_extent, period, period, 1)
    first_row = (jnp.arange(tile_extent) == 0)[:, None]
    alt_t = jnp.where(jnp.arange(period) % 2 == 0, 1.0, -1.0).astype(jnp.float32)[None, :]
    weights = jnp.where(first_row, 1.0, 2.0) / period
    inverse = jnp.concatenate(
        [weights * cos_b, jnp.where(first_row, alt_t / period, -(2.0 / period) * sin_b)], axis=0
    ).astype(jnp.bfloat16)
    return forward, inverse


def filter_spectra(kernel_table_lines, forward, tile_extent):
    lane_total, context_extent = kernel_table_lines.shape
    groups = context_extent // tile_extent
    kernel = (
        kernel_table_lines.astype(jnp.bfloat16)
        .reshape(lane_total, groups, tile_extent)
        .transpose(1, 0, 2)
        .reshape(groups * lane_total, tile_extent)
    )
    spec_k = jnp.dot(kernel, forward, preferred_element_type=jnp.float32)
    return spec_k.reshape(groups, lane_total, 2 * tile_extent)


def global_causal_smear(gate_wave, spec_k, leftover_lines, forward, inverse, tile_extent):
    lane_total, context_extent = gate_wave.shape
    groups = context_extent // tile_extent
    slot0 = (jnp.arange(tile_extent) == 0)[None, None, :]
    source = gate_wave.reshape(lane_total * groups, tile_extent)
    spec_x = jnp.dot(source, forward, preferred_element_type=jnp.float32)
    spec_x = spec_x.reshape(lane_total, groups, 2 * tile_extent)
    x_re, x_im = spec_x[:, :, :tile_extent], spec_x[:, :, tile_extent:]
    k_re, k_im = spec_k[:, :, :tile_extent], spec_k[:, :, tile_extent:]
    pad = jnp.zeros((lane_total, groups - 1, tile_extent), jnp.float32)
    xp_re = jnp.concatenate([pad, x_re], axis=1)
    xp_im = jnp.concatenate([pad, x_im], axis=1)
    rr = ii = ri = ir = None
    for offset in range(groups):
        s_re = xp_re[:, groups - 1 - offset : 2 * groups - 1 - offset]
        s_im = xp_im[:, groups - 1 - offset : 2 * groups - 1 - offset]
        f_re = k_re[offset][:, None, :]
        f_im = k_im[offset][:, None, :]
        terms = (f_re * s_re, f_im * s_im, f_re * s_im, f_im * s_re)
        if rr is None:
            rr, ii, ri, ir = terms
        else:
            rr, ii, ri, ir = rr + terms[0], ii + terms[1], ri + terms[2], ir + terms[3]
    y_re = rr - jnp.where(slot0, 0.0, ii)
    y_im = jnp.where(slot0, ii, ri + ir)
    packed = jnp.concatenate([y_re, y_im], axis=2).astype(jnp.bfloat16)
    rows = jnp.dot(
        packed.reshape(lane_total * groups, 2 * tile_extent),
        inverse,
        preferred_element_type=jnp.float32,
    ).reshape(lane_total, groups, 2 * tile_extent)
    front_half = rows[:, :, :tile_extent]
    back_half = rows[:, :, tile_extent:]
    carried = jnp.concatenate(
        [jnp.zeros((lane_total, 1, tile_extent), jnp.float32), back_half[:, :-1]], axis=1
    )
    affine_mapping = (front_half + carried).reshape(lane_total, context_extent)
    wide = gate_wave.astype(jnp.float32)
    return (affine_mapping + leftover_lines[:, None] * wide).astype(jnp.bfloat16)


def short_conv(projected_float, local_taps, previous):
    context_extent = projected_float.shape[2]
    extended = jnp.concatenate([previous, projected_float], axis=2)
    result = jnp.zeros_like(projected_float)
    for offset in range(3):
        result = (
            result
            + local_taps[:, offset, :][:, :, None]
            * extended[:, :, 2 - offset : 2 - offset + context_extent]
        )
    return result


def make_shards(n_ctx, n_ch, tile_extent):
    def featured(projected, taps):
        local_tokens = projected.shape[2]
        previous = shifted(projected[:, :, local_tokens - 2 :], "ctx", n_ctx, 1)
        return short_conv(projected.astype(jnp.float32), taps, previous.astype(jnp.float32))

    def shards(tokens, in_weight, short_taps, long_filter, skip_gain):
        local_tokens, local_features = tokens.shape
        copies = jnp.broadcast_to(tokens[None], (n_ch, local_tokens, local_features))
        pieces = lax.all_to_all(copies, "ch", split_axis=0, concat_axis=0, tiled=True)
        whole_tokens = pieces.transpose(1, 0, 2).reshape(local_tokens, n_ch * local_features)
        whole_weight = lax.all_gather(in_weight, "ctx", axis=1, tiled=True)
        forward, inverse = spectral_tables(tile_extent)
        spec_k = filter_spectra(long_filter[0], forward, tile_extent)
        whole_weight, forward, inverse, spec_k = lax.optimization_barrier(
            (whole_weight, forward, inverse, spec_k)
        )
        summed = jnp.einsum(
            "pdc,ld->pcl", whole_weight, whole_tokens, preferred_element_type=jnp.float32
        )
        embedding_result = featured(summed.astype(jnp.bfloat16), short_taps)
        gate_wave = (embedding_result[1] * embedding_result[2]).astype(jnp.bfloat16)
        per_channel_view = lax.all_to_all(gate_wave, "ctx", split_axis=0, concat_axis=1, tiled=True)
        blended_lines = global_causal_smear(
            per_channel_view, spec_k, skip_gain[0], forward, inverse, tile_extent
        )
        lanes, span = blended_lines.shape
        outgoing = blended_lines.reshape(lanes, n_ctx, span // n_ctx).transpose(1, 0, 2)
        returned = lax.all_to_all(outgoing, "ctx", split_axis=0, concat_axis=0, tiled=True)
        by_token = returned.reshape(n_ctx * lanes, span // n_ctx)
        gated_output = (embedding_result[0] * by_token.astype(jnp.float32)).astype(jnp.bfloat16)
        return gated_output

    return shards


def solution(mesh):
    placed = (
        P("ctx", "ch"),
        P(None, "ctx", "ch"),
        P(None, None, "ch"),
        P("ch", "ctx", None),
        P("ch", "ctx"),
    )
    return jax.shard_map(
        make_shards(mesh.shape["ctx"], mesh.shape["ch"], BLOCK),
        mesh=mesh,
        in_specs=placed,
        out_specs=P("ch", "ctx"),
        check_vma=False,
    )
```

```python
import math

import jax
import jax.numpy as jnp
from jax import lax
import numpy as np
from jax.sharding import Mesh, NamedSharding
from jax.sharding import PartitionSpec as P

BLOCK = 1024
FACTOR = 32


def shifted(block, axis, size, distance):
    route = [(i - distance, i) for i in range(size) if 0 <= i - distance < size]
    return lax.ppermute(block, axis, route)


def unit_wave(rows, cols, period, scale_rows):
    outer = rows // FACTOR
    hi = jnp.arange(outer, dtype=jnp.int32)[:, None] * (FACTOR * scale_rows)
    lo = jnp.arange(FACTOR, dtype=jnp.int32)[:, None] * scale_rows
    col = jnp.arange(cols, dtype=jnp.int32)[None, :]
    step = 2.0 * math.pi / period
    hi_phase = step * ((hi * col) % period).astype(jnp.float32)
    lo_phase = step * ((lo * col) % period).astype(jnp.float32)
    hc, hs = jnp.cos(hi_phase)[:, None, :], jnp.sin(hi_phase)[:, None, :]
    lc, ls = jnp.cos(lo_phase)[None, :, :], jnp.sin(lo_phase)[None, :, :]
    cos_t = (hc * lc - hs * ls).reshape(rows, cols)
    sin_t = (hs * lc + hc * ls).reshape(rows, cols)
    return cos_t, sin_t


def spectral_tables(tile_extent):
    period = 2 * tile_extent
    cos_f, sin_f = unit_wave(tile_extent, tile_extent, period, 1)
    alternating = jnp.where(jnp.arange(tile_extent) % 2 == 0, 1.0, -1.0).astype(jnp.float32)
    first_col = (jnp.arange(tile_extent) == 0)[None, :]
    forward = jnp.concatenate(
        [cos_f, jnp.where(first_col, alternating[:, None], -sin_f)], axis=1
    ).astype(jnp.bfloat16)
    cos_b, sin_b = unit_wave(tile_extent, period, period, 1)
    first_row = (jnp.arange(tile_extent) == 0)[:, None]
    alt_t = jnp.where(jnp.arange(period) % 2 == 0, 1.0, -1.0).astype(jnp.float32)[None, :]
    weights = jnp.where(first_row, 1.0, 2.0) / period
    inverse = jnp.concatenate(
        [weights * cos_b, jnp.where(first_row, alt_t / period, -(2.0 / period) * sin_b)], axis=0
    ).astype(jnp.bfloat16)
    return forward, inverse


def filter_spectra(kernel_table_lines, forward, tile_extent):
    lane_total, context_extent = kernel_table_lines.shape
    groups = context_extent // tile_extent
    kernel = (
        kernel_table_lines.astype(jnp.bfloat16)
        .reshape(lane_total, groups, tile_extent)
        .transpose(1, 0, 2)
        .reshape(groups * lane_total, tile_extent)
    )
    spec_k = jnp.dot(kernel, forward, preferred_element_type=jnp.float32)
    return spec_k.reshape(groups, lane_total, 2 * tile_extent)


def global_causal_smear(gate_wave, spec_k, leftover_lines, forward, inverse, tile_extent):
    lane_total, context_extent = gate_wave.shape
    groups = context_extent // tile_extent
    slot0 = (jnp.arange(tile_extent) == 0)[None, None, :]
    source = gate_wave.reshape(lane_total * groups, tile_extent)
    spec_x = jnp.dot(source, forward, preferred_element_type=jnp.float32)
    spec_x = spec_x.reshape(lane_total, groups, 2 * tile_extent)
    x_re, x_im = spec_x[:, :, :tile_extent], spec_x[:, :, tile_extent:]
    k_re, k_im = spec_k[:, :, :tile_extent], spec_k[:, :, tile_extent:]
    pad = jnp.zeros((lane_total, groups - 1, tile_extent), jnp.float32)
    xp_re = jnp.concatenate([pad, x_re], axis=1)
    xp_im = jnp.concatenate([pad, x_im], axis=1)
    rr = ii = ri = ir = None
    for offset in range(groups):
        s_re = xp_re[:, groups - 1 - offset : 2 * groups - 1 - offset]
        s_im = xp_im[:, groups - 1 - offset : 2 * groups - 1 - offset]
        f_re = k_re[offset][:, None, :]
        f_im = k_im[offset][:, None, :]
        terms = (f_re * s_re, f_im * s_im, f_re * s_im, f_im * s_re)
        if rr is None:
            rr, ii, ri, ir = terms
        else:
            rr, ii, ri, ir = rr + terms[0], ii + terms[1], ri + terms[2], ir + terms[3]
    y_re = rr - jnp.where(slot0, 0.0, ii)
    y_im = jnp.where(slot0, ii, ri + ir)
    packed = jnp.concatenate([y_re, y_im], axis=2).astype(jnp.bfloat16)
    rows = jnp.dot(
        packed.reshape(lane_total * groups, 2 * tile_extent),
        inverse,
        preferred_element_type=jnp.float32,
    ).reshape(lane_total, groups, 2 * tile_extent)
    front_half = rows[:, :, :tile_extent]
    back_half = rows[:, :, tile_extent:]
    carried = jnp.concatenate(
        [jnp.zeros((lane_total, 1, tile_extent), jnp.float32), back_half[:, :-1]], axis=1
    )
    affine_mapping = (front_half + carried).reshape(lane_total, context_extent)
    wide = gate_wave.astype(jnp.float32)
    return (affine_mapping + leftover_lines[:, None] * wide).astype(jnp.bfloat16)


def short_conv(projected_float, local_taps, previous):
    context_extent = projected_float.shape[2]
    extended = jnp.concatenate([previous, projected_float], axis=2)
    result = jnp.zeros_like(projected_float)
    for offset in range(3):
        result = (
            result
            + local_taps[:, offset, :][:, :, None]
            * extended[:, :, 2 - offset : 2 - offset + context_extent]
        )
    return result


def make_shards(n_ctx, n_ch, tile_extent):
    ctx = ("yh", "cq")
    swap = [(0, 1), (1, 0)]

    def featured(projected, taps):
        local_tokens = projected.shape[2]
        previous = shifted(projected[:, :, local_tokens - 2 :], ctx, n_ctx, 1)
        return short_conv(projected.astype(jnp.float32), taps, previous.astype(jnp.float32))

    def by_half(half, own, other):
        first = jnp.where(half == 0, own, other)
        second = jnp.where(half == 0, other, own)
        return jnp.stack([first, second])

    def shards(tokens, in_weight, short_taps, long_filter, skip_gain):
        half = lax.axis_index("yh")
        local_tokens, local_features = tokens.shape
        branches, local_rows, lanes = in_weight.shape
        width = lanes // 2
        own_cols = lax.dynamic_slice_in_dim(in_weight, half * width, width, axis=2)
        other_cols = lax.dynamic_slice_in_dim(in_weight, (1 - half) * width, width, axis=2)
        partner_rows = lax.ppermute(other_cols, "yh", swap)
        rows_pair = by_half(half, own_cols, partner_rows)
        gathered = lax.all_gather(rows_pair, "cq", axis=0, tiled=False)
        whole_weight = gathered.transpose(2, 0, 1, 3, 4).reshape(branches, -1, width)
        partner_tokens = lax.ppermute(tokens, "yh", swap)
        token_pair = by_half(half, tokens, partner_tokens)
        copies = jnp.broadcast_to(token_pair[None], (n_ch,) + token_pair.shape)
        pieces = lax.all_to_all(copies, "ch", split_axis=0, concat_axis=0, tiled=True)
        n_q = n_ctx // 2
        whole_tokens = (
            pieces.transpose(1, 2, 0, 3)
            .reshape(2 * local_tokens, 2, n_q, local_rows)
            .transpose(0, 2, 1, 3)
            .reshape(2 * local_tokens, -1)
        )
        forward, inverse = spectral_tables(tile_extent)
        spec_k = filter_spectra(long_filter[0], forward, tile_extent)
        whole_weight, forward, inverse, spec_k = lax.optimization_barrier(
            (whole_weight, forward, inverse, spec_k)
        )
        summed = jnp.einsum(
            "pdc,ld->pcl", whole_weight, whole_tokens, preferred_element_type=jnp.float32
        ).astype(jnp.bfloat16)
        own_part = lax.dynamic_slice_in_dim(summed, half * local_tokens, local_tokens, axis=2)
        other_part = lax.dynamic_slice_in_dim(summed, (1 - half) * local_tokens, local_tokens, axis=2)
        received = lax.ppermute(other_part, "yh", swap)
        projected = jnp.concatenate(list(by_half(half, own_part, received)), axis=1)
        embedding_result = featured(projected, short_taps)
        gate_wave = (embedding_result[1] * embedding_result[2]).astype(jnp.bfloat16)
        per_channel_view = lax.all_to_all(gate_wave, ctx, split_axis=0, concat_axis=1, tiled=True)
        blended_lines = global_causal_smear(
            per_channel_view, spec_k, skip_gain[0], forward, inverse, tile_extent
        )
        lines, span = blended_lines.shape
        outgoing = blended_lines.reshape(lines, n_ctx, span // n_ctx).transpose(1, 0, 2)
        returned = lax.all_to_all(outgoing, ctx, split_axis=0, concat_axis=0, tiled=True)
        by_token = returned.reshape(n_ctx * lines, span // n_ctx)
        gated_output = (embedding_result[0] * by_token.astype(jnp.float32)).astype(jnp.bfloat16)
        return gated_output

    return shards


def solution(mesh):
    n_ctx = mesh.shape["ctx"]
    grid = np.asarray(mesh.devices).reshape(2, n_ctx // 2, mesh.shape["ch"])
    split_mesh = Mesh(grid, ("yh", "cq", "ch"))
    ctx = ("yh", "cq")
    placed = (
        P(ctx, "ch"),
        P(None, ctx, "ch"),
        P(None, None, "ch"),
        P("ch", ctx, None),
        P("ch", ctx),
    )
    mapped = jax.shard_map(
        make_shards(n_ctx, mesh.shape["ch"], BLOCK),
        mesh=split_mesh,
        in_specs=placed,
        out_specs=P("ch", ctx),
        check_vma=False,
    )
    out_sharding = NamedSharding(mesh, P("ch", "ctx"))

    def run(*args):
        return lax.with_sharding_constraint(mapped(*args), out_sharding)

    return run
```

```python
import math

import jax
import jax.numpy as jnp
from jax import lax
import numpy as np
from jax.sharding import Mesh, NamedSharding
from jax.sharding import PartitionSpec as P

BLOCK = 1024
FACTOR = 32


def shifted(block, axis, size, distance):
    route = [(i - distance, i) for i in range(size) if 0 <= i - distance < size]
    return lax.ppermute(block, axis, route)


def unit_wave(rows, cols, period, scale_rows):
    outer = rows // FACTOR
    hi = jnp.arange(outer, dtype=jnp.int32)[:, None] * (FACTOR * scale_rows)
    lo = jnp.arange(FACTOR, dtype=jnp.int32)[:, None] * scale_rows
    col = jnp.arange(cols, dtype=jnp.int32)[None, :]
    step = 2.0 * math.pi / period
    hi_phase = step * ((hi * col) % period).astype(jnp.float32)
    lo_phase = step * ((lo * col) % period).astype(jnp.float32)
    hc, hs = jnp.cos(hi_phase)[:, None, :], jnp.sin(hi_phase)[:, None, :]
    lc, ls = jnp.cos(lo_phase)[None, :, :], jnp.sin(lo_phase)[None, :, :]
    cos_t = (hc * lc - hs * ls).reshape(rows, cols)
    sin_t = (hs * lc + hc * ls).reshape(rows, cols)
    return cos_t, sin_t


def spectral_tables(tile_extent):
    period = 2 * tile_extent
    cos_f, sin_f = unit_wave(tile_extent, tile_extent, period, 1)
    alternating = jnp.where(jnp.arange(tile_extent) % 2 == 0, 1.0, -1.0).astype(jnp.float32)
    first_col = (jnp.arange(tile_extent) == 0)[None, :]
    forward = jnp.concatenate(
        [cos_f, jnp.where(first_col, alternating[:, None], -sin_f)], axis=1
    ).astype(jnp.bfloat16)
    cos_b, sin_b = unit_wave(tile_extent, period, period, 1)
    first_row = (jnp.arange(tile_extent) == 0)[:, None]
    alt_t = jnp.where(jnp.arange(period) % 2 == 0, 1.0, -1.0).astype(jnp.float32)[None, :]
    weights = jnp.where(first_row, 1.0, 2.0) / period
    inverse = jnp.concatenate(
        [weights * cos_b, jnp.where(first_row, alt_t / period, -(2.0 / period) * sin_b)], axis=0
    ).astype(jnp.bfloat16)
    return forward, inverse


def filter_spectra(kernel_table_lines, forward, tile_extent):
    lane_total, context_extent = kernel_table_lines.shape
    groups = context_extent // tile_extent
    kernel = (
        kernel_table_lines.astype(jnp.bfloat16)
        .reshape(lane_total, groups, tile_extent)
        .transpose(1, 0, 2)
        .reshape(groups * lane_total, tile_extent)
    )
    spec_k = jnp.dot(kernel, forward, preferred_element_type=jnp.float32)
    return spec_k.reshape(groups, lane_total, 2 * tile_extent)


def global_causal_smear(gate_wave, spec_k, leftover_lines, forward, inverse, tile_extent):
    lane_total, context_extent = gate_wave.shape
    groups = context_extent // tile_extent
    slot0 = (jnp.arange(tile_extent) == 0)[None, None, :]
    source = gate_wave.reshape(lane_total * groups, tile_extent)
    spec_x = jnp.dot(source, forward, preferred_element_type=jnp.float32)
    spec_x = spec_x.reshape(lane_total, groups, 2 * tile_extent)
    x_re, x_im = spec_x[:, :, :tile_extent], spec_x[:, :, tile_extent:]
    k_re, k_im = spec_k[:, :, :tile_extent], spec_k[:, :, tile_extent:]
    pad = jnp.zeros((lane_total, groups - 1, tile_extent), jnp.float32)
    xp_re = jnp.concatenate([pad, x_re], axis=1)
    xp_im = jnp.concatenate([pad, x_im], axis=1)
    rr = ii = ri = ir = None
    for offset in range(groups):
        s_re = xp_re[:, groups - 1 - offset : 2 * groups - 1 - offset]
        s_im = xp_im[:, groups - 1 - offset : 2 * groups - 1 - offset]
        f_re = k_re[offset][:, None, :]
        f_im = k_im[offset][:, None, :]
        terms = (f_re * s_re, f_im * s_im, f_re * s_im, f_im * s_re)
        if rr is None:
            rr, ii, ri, ir = terms
        else:
            rr, ii, ri, ir = rr + terms[0], ii + terms[1], ri + terms[2], ir + terms[3]
    y_re = rr - jnp.where(slot0, 0.0, ii)
    y_im = jnp.where(slot0, ii, ri + ir)
    packed = jnp.concatenate([y_re, y_im], axis=2).astype(jnp.bfloat16)
    rows = jnp.dot(
        packed.reshape(lane_total * groups, 2 * tile_extent),
        inverse,
        preferred_element_type=jnp.float32,
    ).reshape(lane_total, groups, 2 * tile_extent)
    front_half = rows[:, :, :tile_extent]
    back_half = rows[:, :, tile_extent:]
    carried = jnp.concatenate(
        [jnp.zeros((lane_total, 1, tile_extent), jnp.float32), back_half[:, :-1]], axis=1
    )
    affine_mapping = (front_half + carried).reshape(lane_total, context_extent)
    wide = gate_wave.astype(jnp.float32)
    return (affine_mapping + leftover_lines[:, None] * wide).astype(jnp.bfloat16)


def short_conv(projected_float, local_taps, previous):
    context_extent = projected_float.shape[2]
    extended = jnp.concatenate([previous, projected_float], axis=2)
    result = jnp.zeros_like(projected_float)
    for offset in range(3):
        result = (
            result
            + local_taps[:, offset, :][:, :, None]
            * extended[:, :, 2 - offset : 2 - offset + context_extent]
        )
    return result


def make_shards(n_ctx, n_ch, tile_extent):
    ctx = ("yh", "cq")
    swap = [(0, 1), (1, 0)]

    def featured(projected, taps):
        local_tokens = projected.shape[2]
        previous = shifted(projected[:, :, local_tokens - 2 :], ctx, n_ctx, 1)
        return short_conv(projected.astype(jnp.float32), taps, previous.astype(jnp.float32))

    def by_half(half, own, other):
        first = jnp.where(half == 0, own, other)
        second = jnp.where(half == 0, other, own)
        return jnp.stack([first, second])

    def shards(tokens, in_weight, short_taps, long_filter, skip_gain):
        half = lax.axis_index("yh")
        local_tokens, local_features = tokens.shape
        branches, local_rows, lanes = in_weight.shape
        width = lanes // 2
        own_cols = lax.dynamic_slice_in_dim(in_weight, half * width, width, axis=2)
        other_cols = lax.dynamic_slice_in_dim(in_weight, (1 - half) * width, width, axis=2)
        partner_rows = lax.ppermute(other_cols, "yh", swap)
        rows_pair = jnp.stack(list(by_half(half, own_cols, partner_rows)), axis=1)
        gathered = lax.all_gather(rows_pair, "cq", axis=2, tiled=False)
        whole_weight = gathered.reshape(branches, -1, width)
        partner_tokens = lax.ppermute(tokens, "yh", swap)
        token_pair = by_half(half, tokens, partner_tokens)
        copies = jnp.broadcast_to(token_pair[None], (n_ch,) + token_pair.shape)
        pieces = lax.all_to_all(copies, "ch", split_axis=0, concat_axis=3, tiled=True)
        whole_tokens = pieces.reshape(2 * local_tokens, n_ch * local_features)
        forward, inverse = spectral_tables(tile_extent)
        spec_k = filter_spectra(long_filter[0], forward, tile_extent)
        whole_weight, forward, inverse, spec_k = lax.optimization_barrier(
            (whole_weight, forward, inverse, spec_k)
        )
        summed = jnp.einsum(
            "pdc,ld->pcl", whole_weight, whole_tokens, preferred_element_type=jnp.float32
        ).astype(jnp.bfloat16)
        own_part = lax.dynamic_slice_in_dim(summed, half * local_tokens, local_tokens, axis=2)
        other_part = lax.dynamic_slice_in_dim(summed, (1 - half) * local_tokens, local_tokens, axis=2)
        received = lax.ppermute(other_part, "yh", swap)
        projected = jnp.concatenate(list(by_half(half, own_part, received)), axis=1)
        embedding_result = featured(projected, short_taps)
        gate_wave = (embedding_result[1] * embedding_result[2]).astype(jnp.bfloat16)
        per_channel_view = lax.all_to_all(gate_wave, ctx, split_axis=0, concat_axis=1, tiled=True)
        blended_lines = global_causal_smear(
            per_channel_view, spec_k, skip_gain[0], forward, inverse, tile_extent
        )
        lines, span = blended_lines.shape
        outgoing = blended_lines.reshape(lines, n_ctx, span // n_ctx).transpose(1, 0, 2)
        returned = lax.all_to_all(outgoing, ctx, split_axis=0, concat_axis=0, tiled=True)
        by_token = returned.reshape(n_ctx * lines, span // n_ctx)
        gated_output = (embedding_result[0] * by_token.astype(jnp.float32)).astype(jnp.bfloat16)
        return gated_output

    return shards


def solution(mesh):
    n_ctx = mesh.shape["ctx"]
    grid = np.asarray(mesh.devices).reshape(2, n_ctx // 2, mesh.shape["ch"])
    split_mesh = Mesh(grid, ("yh", "cq", "ch"))
    ctx = ("yh", "cq")
    placed = (
        P(ctx, "ch"),
        P(None, ctx, "ch"),
        P(None, None, "ch"),
        P("ch", ctx, None),
        P("ch", ctx),
    )
    mapped = jax.shard_map(
        make_shards(n_ctx, mesh.shape["ch"], BLOCK),
        mesh=split_mesh,
        in_specs=placed,
        out_specs=P("ch", ctx),
        check_vma=False,
    )
    out_sharding = NamedSharding(mesh, P("ch", "ctx"))

    def run(*args):
        return lax.with_sharding_constraint(mapped(*args), out_sharding)

    return run
```

```python
import math

import jax
import jax.numpy as jnp
from jax import lax
import numpy as np
from jax.sharding import Mesh, NamedSharding
from jax.sharding import PartitionSpec as P

BLOCK = 1024
FACTOR = 32


def shifted(block, axis, size, distance):
    route = [(i - distance, i) for i in range(size) if 0 <= i - distance < size]
    return lax.ppermute(block, axis, route)


def unit_wave(rows, cols, period, scale_rows):
    outer = rows // FACTOR
    hi = jnp.arange(outer, dtype=jnp.int32)[:, None] * (FACTOR * scale_rows)
    lo = jnp.arange(FACTOR, dtype=jnp.int32)[:, None] * scale_rows
    col = jnp.arange(cols, dtype=jnp.int32)[None, :]
    step = 2.0 * math.pi / period
    hi_phase = step * ((hi * col) % period).astype(jnp.float32)
    lo_phase = step * ((lo * col) % period).astype(jnp.float32)
    hc, hs = jnp.cos(hi_phase)[:, None, :], jnp.sin(hi_phase)[:, None, :]
    lc, ls = jnp.cos(lo_phase)[None, :, :], jnp.sin(lo_phase)[None, :, :]
    cos_t = (hc * lc - hs * ls).reshape(rows, cols)
    sin_t = (hs * lc + hc * ls).reshape(rows, cols)
    return cos_t, sin_t


def spectral_tables(tile_extent):
    period = 2 * tile_extent
    cos_f, sin_f = unit_wave(tile_extent, tile_extent, period, 1)
    alternating = jnp.where(jnp.arange(tile_extent) % 2 == 0, 1.0, -1.0).astype(jnp.float32)
    first_col = (jnp.arange(tile_extent) == 0)[None, :]
    forward = jnp.concatenate(
        [cos_f, jnp.where(first_col, alternating[:, None], -sin_f)], axis=1
    ).astype(jnp.bfloat16)
    cos_b, sin_b = unit_wave(tile_extent, period, period, 1)
    first_row = (jnp.arange(tile_extent) == 0)[:, None]
    alt_t = jnp.where(jnp.arange(period) % 2 == 0, 1.0, -1.0).astype(jnp.float32)[None, :]
    weights = jnp.where(first_row, 1.0, 2.0) / period
    inverse = jnp.concatenate(
        [weights * cos_b, jnp.where(first_row, alt_t / period, -(2.0 / period) * sin_b)], axis=0
    ).astype(jnp.bfloat16)
    return forward, inverse


def filter_spectra(kernel_table_lines, forward, tile_extent):
    lane_total, context_extent = kernel_table_lines.shape
    groups = context_extent // tile_extent
    kernel = (
        kernel_table_lines.astype(jnp.bfloat16)
        .reshape(lane_total, groups, tile_extent)
        .transpose(1, 0, 2)
        .reshape(groups * lane_total, tile_extent)
    )
    spec_k = jnp.dot(kernel, forward, preferred_element_type=jnp.float32)
    return spec_k.reshape(groups, lane_total, 2 * tile_extent)


def global_causal_smear(gate_wave, spec_k, leftover_lines, forward, inverse, tile_extent):
    lane_total, context_extent = gate_wave.shape
    groups = context_extent // tile_extent
    slot0 = (jnp.arange(tile_extent) == 0)[None, None, :]
    source = gate_wave.reshape(lane_total * groups, tile_extent)
    spec_x = jnp.dot(source, forward, preferred_element_type=jnp.float32)
    spec_x = spec_x.reshape(lane_total, groups, 2 * tile_extent)
    x_re, x_im = spec_x[:, :, :tile_extent], spec_x[:, :, tile_extent:]
    k_re, k_im = spec_k[:, :, :tile_extent], spec_k[:, :, tile_extent:]
    pad = jnp.zeros((lane_total, groups - 1, tile_extent), jnp.float32)
    xp_re = jnp.concatenate([pad, x_re], axis=1)
    xp_im = jnp.concatenate([pad, x_im], axis=1)
    rr = ii = ri = ir = None
    for offset in range(groups):
        s_re = xp_re[:, groups - 1 - offset : 2 * groups - 1 - offset]
        s_im = xp_im[:, groups - 1 - offset : 2 * groups - 1 - offset]
        f_re = k_re[offset][:, None, :]
        f_im = k_im[offset][:, None, :]
        terms = (f_re * s_re, f_im * s_im, f_re * s_im, f_im * s_re)
        if rr is None:
            rr, ii, ri, ir = terms
        else:
            rr, ii, ri, ir = rr + terms[0], ii + terms[1], ri + terms[2], ir + terms[3]
    y_re = rr - jnp.where(slot0, 0.0, ii)
    y_im = jnp.where(slot0, ii, ri + ir)
    packed = jnp.concatenate([y_re, y_im], axis=2).astype(jnp.bfloat16)
    rows = jnp.dot(
        packed.reshape(lane_total * groups, 2 * tile_extent),
        inverse,
        preferred_element_type=jnp.float32,
    ).reshape(lane_total, groups, 2 * tile_extent)
    front_half = rows[:, :, :tile_extent]
    back_half = rows[:, :, tile_extent:]
    carried = jnp.concatenate(
        [jnp.zeros((lane_total, 1, tile_extent), jnp.float32), back_half[:, :-1]], axis=1
    )
    affine_mapping = (front_half + carried).reshape(lane_total, context_extent)
    wide = gate_wave.astype(jnp.float32)
    return (affine_mapping + leftover_lines[:, None] * wide).astype(jnp.bfloat16)


def short_conv(projected_float, local_taps, previous):
    context_extent = projected_float.shape[2]
    extended = jnp.concatenate([previous, projected_float], axis=2)
    result = jnp.zeros_like(projected_float)
    for offset in range(3):
        result = (
            result
            + local_taps[:, offset, :][:, :, None]
            * extended[:, :, 2 - offset : 2 - offset + context_extent]
        )
    return result


def make_shards(n_ctx, n_ch, tile_extent):
    ctx = ("yh", "cq")
    swap = [(0, 1), (1, 0)]

    def featured(projected, taps):
        local_tokens = projected.shape[2]
        previous = shifted(projected[:, :, local_tokens - 2 :], ctx, n_ctx, 1)
        return short_conv(projected.astype(jnp.float32), taps, previous.astype(jnp.float32))

    def by_half(half, own, other):
        first = jnp.where(half == 0, own, other)
        second = jnp.where(half == 0, other, own)
        return jnp.stack([first, second])

    def shards(tokens, in_weight, short_taps, long_filter, skip_gain):
        half = lax.axis_index("yh")
        local_tokens, local_features = tokens.shape
        branches, local_rows, lanes = in_weight.shape
        width = lanes // 2
        n_q = n_ctx // 2
        own_cols = lax.dynamic_slice_in_dim(in_weight, half * width, width, axis=2)
        other_cols = lax.dynamic_slice_in_dim(in_weight, (1 - half) * width, width, axis=2)
        partner_rows = lax.ppermute(other_cols, "yh", swap)
        rows_pair = jnp.stack(list(by_half(half, own_cols, partner_rows)), axis=1)
        gathered = lax.all_gather(rows_pair, "cq", axis=2, tiled=False)
        whole_weight = gathered.reshape(branches, -1, width)
        partner_tokens = lax.ppermute(tokens, "yh", swap)
        token_pair = by_half(half, tokens, partner_tokens)
        copies = jnp.broadcast_to(token_pair[None], (n_ch,) + token_pair.shape)
        pieces = lax.all_to_all(copies, "ch", split_axis=0, concat_axis=3, tiled=True)
        whole_tokens = pieces.reshape(2 * local_tokens, n_ch * local_features)
        forward, inverse = spectral_tables(tile_extent)
        spec_k = filter_spectra(long_filter[0], forward, tile_extent)
        whole_weight, forward, inverse, spec_k = lax.optimization_barrier(
            (whole_weight, forward, inverse, spec_k)
        )
        summed = jnp.einsum(
            "pdc,ld->pcl", whole_weight, whole_tokens, preferred_element_type=jnp.float32
        ).astype(jnp.bfloat16)
        own_part = lax.dynamic_slice_in_dim(summed[0:1], half * local_tokens, local_tokens, axis=2)
        other_part = lax.dynamic_slice_in_dim(
            summed[0:1], (1 - half) * local_tokens, local_tokens, axis=2
        )
        received = lax.ppermute(other_part, "yh", swap)
        projected0 = jnp.concatenate(list(by_half(half, own_part, received)), axis=1)
        embed0 = featured(projected0, short_taps[0:1])
        q = lax.axis_index("cq")
        blocks = summed[1:3].reshape(2, width, 2, local_tokens)
        tails = blocks[:, :, :, local_tokens - 2 :]
        ring = [(i, (i + 1) % n_q) for i in range(n_q)]
        arrived = lax.ppermute(tails, "cq", ring)
        first = jnp.concatenate([jnp.zeros_like(arrived[:, :, :1]), arrived[:, :, :1]], axis=2)
        halo = jnp.where(q == 0, first, arrived)
        taps12 = lax.dynamic_slice_in_dim(short_taps[1:3], half * width, width, axis=2)
        extended = jnp.concatenate([halo, blocks], axis=3).astype(jnp.float32)
        embed12 = None
        for offset in range(3):
            term = taps12[:, offset, :][:, :, None, None] * extended[
                :, :, :, 2 - offset : 2 - offset + local_tokens
            ]
            embed12 = term if embed12 is None else embed12 + term
        gate_wave = (embed12[0] * embed12[1]).astype(jnp.bfloat16)
        lanes_each = width // n_q
        outgoing12 = gate_wave.reshape(n_q, lanes_each, 2, local_tokens)
        got = lax.all_to_all(outgoing12, "cq", split_axis=0, concat_axis=0, tiled=True)
        per_channel_view = got.transpose(1, 2, 0, 3).reshape(lanes_each, -1)
        blended_lines = global_causal_smear(
            per_channel_view, spec_k, skip_gain[0], forward, inverse, tile_extent
        )
        lines, span = blended_lines.shape
        outgoing = blended_lines.reshape(lines, n_ctx, span // n_ctx).transpose(1, 0, 2)
        returned = lax.all_to_all(outgoing, ctx, split_axis=0, concat_axis=0, tiled=True)
        by_token = returned.reshape(n_ctx * lines, span // n_ctx)
        gated_output = (embed0[0] * by_token.astype(jnp.float32)).astype(jnp.bfloat16)
        return gated_output

    return shards


def solution(mesh):
    n_ctx = mesh.shape["ctx"]
    grid = np.asarray(mesh.devices).reshape(2, n_ctx // 2, mesh.shape["ch"])
    split_mesh = Mesh(grid, ("yh", "cq", "ch"))
    ctx = ("yh", "cq")
    placed = (
        P(ctx, "ch"),
        P(None, ctx, "ch"),
        P(None, None, "ch"),
        P("ch", ctx, None),
        P("ch", ctx),
    )
    mapped = jax.shard_map(
        make_shards(n_ctx, mesh.shape["ch"], BLOCK),
        mesh=split_mesh,
        in_specs=placed,
        out_specs=P("ch", ctx),
        check_vma=False,
    )
    out_sharding = NamedSharding(mesh, P("ch", "ctx"))

    def run(*args):
        return lax.with_sharding_constraint(mapped(*args), out_sharding)

    return run
```

```python
import math

import jax
import jax.numpy as jnp
from jax import lax
import numpy as np
from jax.sharding import Mesh, NamedSharding
from jax.sharding import PartitionSpec as P

BLOCK = 1024
FACTOR = 32


def shifted(block, axis, size, distance):
    route = [(i - distance, i) for i in range(size) if 0 <= i - distance < size]
    return lax.ppermute(block, axis, route)


def unit_wave(rows, cols, period, scale_rows):
    outer = rows // FACTOR
    hi = jnp.arange(outer, dtype=jnp.int32)[:, None] * (FACTOR * scale_rows)
    lo = jnp.arange(FACTOR, dtype=jnp.int32)[:, None] * scale_rows
    col = jnp.arange(cols, dtype=jnp.int32)[None, :]
    step = 2.0 * math.pi / period
    hi_phase = step * ((hi * col) % period).astype(jnp.float32)
    lo_phase = step * ((lo * col) % period).astype(jnp.float32)
    hc, hs = jnp.cos(hi_phase)[:, None, :], jnp.sin(hi_phase)[:, None, :]
    lc, ls = jnp.cos(lo_phase)[None, :, :], jnp.sin(lo_phase)[None, :, :]
    cos_t = (hc * lc - hs * ls).reshape(rows, cols)
    sin_t = (hs * lc + hc * ls).reshape(rows, cols)
    return cos_t, sin_t


def spectral_tables(tile_extent):
    period = 2 * tile_extent
    cos_f, sin_f = unit_wave(tile_extent, tile_extent, period, 1)
    alternating = jnp.where(jnp.arange(tile_extent) % 2 == 0, 1.0, -1.0).astype(jnp.float32)
    first_col = (jnp.arange(tile_extent) == 0)[None, :]
    forward = jnp.concatenate(
        [cos_f, jnp.where(first_col, alternating[:, None], -sin_f)], axis=1
    ).astype(jnp.bfloat16)
    cos_b, sin_b = unit_wave(tile_extent, period, period, 1)
    first_row = (jnp.arange(tile_extent) == 0)[:, None]
    alt_t = jnp.where(jnp.arange(period) % 2 == 0, 1.0, -1.0).astype(jnp.float32)[None, :]
    weights = jnp.where(first_row, 1.0, 2.0) / period
    inverse = jnp.concatenate(
        [weights * cos_b, jnp.where(first_row, alt_t / period, -(2.0 / period) * sin_b)], axis=0
    ).astype(jnp.bfloat16)
    return forward, inverse


def filter_spectra(kernel_table_lines, forward, tile_extent):
    lane_total, context_extent = kernel_table_lines.shape
    groups = context_extent // tile_extent
    kernel = (
        kernel_table_lines.astype(jnp.bfloat16)
        .reshape(lane_total, groups, tile_extent)
        .transpose(1, 0, 2)
        .reshape(groups * lane_total, tile_extent)
    )
    spec_k = jnp.dot(kernel, forward, preferred_element_type=jnp.float32)
    return spec_k.reshape(groups, lane_total, 2 * tile_extent)


def global_causal_smear(gate_wave, spec_k, leftover_lines, forward, inverse, tile_extent):
    lane_total, context_extent = gate_wave.shape
    groups = context_extent // tile_extent
    slot0 = (jnp.arange(tile_extent) == 0)[None, None, :]
    source = gate_wave.reshape(lane_total * groups, tile_extent)
    spec_x = jnp.dot(source, forward, preferred_element_type=jnp.float32)
    spec_x = spec_x.reshape(lane_total, groups, 2 * tile_extent)
    x_re, x_im = spec_x[:, :, :tile_extent], spec_x[:, :, tile_extent:]
    k_re, k_im = spec_k[:, :, :tile_extent], spec_k[:, :, tile_extent:]
    pad = jnp.zeros((lane_total, groups - 1, tile_extent), jnp.float32)
    xp_re = jnp.concatenate([pad, x_re], axis=1)
    xp_im = jnp.concatenate([pad, x_im], axis=1)
    rr = ii = ri = ir = None
    for offset in range(groups):
        s_re = xp_re[:, groups - 1 - offset : 2 * groups - 1 - offset]
        s_im = xp_im[:, groups - 1 - offset : 2 * groups - 1 - offset]
        f_re = k_re[offset][:, None, :]
        f_im = k_im[offset][:, None, :]
        terms = (f_re * s_re, f_im * s_im, f_re * s_im, f_im * s_re)
        if rr is None:
            rr, ii, ri, ir = terms
        else:
            rr, ii, ri, ir = rr + terms[0], ii + terms[1], ri + terms[2], ir + terms[3]
    y_re = rr - jnp.where(slot0, 0.0, ii)
    y_im = jnp.where(slot0, ii, ri + ir)
    packed = jnp.concatenate([y_re, y_im], axis=2).astype(jnp.bfloat16)
    rows = jnp.dot(
        packed.reshape(lane_total * groups, 2 * tile_extent),
        inverse,
        preferred_element_type=jnp.float32,
    ).reshape(lane_total, groups, 2 * tile_extent)
    front_half = rows[:, :, :tile_extent]
    back_half = rows[:, :, tile_extent:]
    carried = jnp.concatenate(
        [jnp.zeros((lane_total, 1, tile_extent), jnp.float32), back_half[:, :-1]], axis=1
    )
    affine_mapping = (front_half + carried).reshape(lane_total, context_extent)
    wide = gate_wave.astype(jnp.float32)
    return (affine_mapping + leftover_lines[:, None] * wide).astype(jnp.bfloat16)


def short_conv(projected_float, local_taps, previous):
    context_extent = projected_float.shape[2]
    extended = jnp.concatenate([previous, projected_float], axis=2)
    result = jnp.zeros_like(projected_float)
    for offset in range(3):
        result = (
            result
            + local_taps[:, offset, :][:, :, None]
            * extended[:, :, 2 - offset : 2 - offset + context_extent]
        )
    return result


def make_shards(n_ctx, n_ch, tile_extent):
    ctx = ("yh", "cq")
    swap = [(0, 1), (1, 0)]

    def featured(projected, taps):
        local_tokens = projected.shape[2]
        previous = shifted(projected[:, :, local_tokens - 2 :], ctx, n_ctx, 1)
        return short_conv(projected.astype(jnp.float32), taps, previous.astype(jnp.float32))

    def by_half(half, own, other):
        first = jnp.where(half == 0, own, other)
        second = jnp.where(half == 0, other, own)
        return jnp.stack([first, second])

    def shards(tokens, in_weight, short_taps, long_filter, skip_gain):
        half = lax.axis_index("yh")
        local_tokens, local_features = tokens.shape
        branches, local_rows, lanes = in_weight.shape
        width = lanes // 2
        n_q = n_ctx // 2
        own_cols = lax.dynamic_slice_in_dim(in_weight, half * width, width, axis=2)
        other_cols = lax.dynamic_slice_in_dim(in_weight, (1 - half) * width, width, axis=2)
        partner_rows = lax.ppermute(other_cols, "yh", swap)
        rows_pair = jnp.stack(list(by_half(half, own_cols, partner_rows)), axis=1)
        gathered = lax.all_gather(rows_pair, "cq", axis=2, tiled=False)
        whole_weight = gathered.reshape(branches, -1, width)
        partner_tokens = lax.ppermute(tokens, "yh", swap)
        token_pair = by_half(half, tokens, partner_tokens)
        copies = jnp.broadcast_to(token_pair[None], (n_ch,) + token_pair.shape)
        pieces = lax.all_to_all(copies, "ch", split_axis=0, concat_axis=3, tiled=True)
        whole_tokens = pieces.reshape(2 * local_tokens, n_ch * local_features)
        forward, inverse = spectral_tables(tile_extent)
        spec_k = filter_spectra(long_filter[0], forward, tile_extent)
        whole_weight, forward, inverse, spec_k = lax.optimization_barrier(
            (whole_weight, forward, inverse, spec_k)
        )
        summed = jnp.einsum(
            "pdc,ld->pcl", whole_weight, whole_tokens, preferred_element_type=jnp.float32
        ).astype(jnp.bfloat16)
        own_part = lax.dynamic_slice_in_dim(summed[0:1], half * local_tokens, local_tokens, axis=2)
        other_part = lax.dynamic_slice_in_dim(
            summed[0:1], (1 - half) * local_tokens, local_tokens, axis=2
        )
        received = lax.ppermute(other_part, "yh", swap)
        q = lax.axis_index("cq")
        blocks = summed[1:3].reshape(2, width, 2, local_tokens)
        tails = blocks[:, :, :, local_tokens - 2 :].transpose(0, 2, 3, 1).reshape(-1, width)
        ring = [(i, (i + 1) % n_q) for i in range(n_q)]
        arrived = lax.ppermute(tails, "cq", ring).reshape(2, 2, 2, width).transpose(0, 3, 1, 2)
        first = jnp.concatenate([jnp.zeros_like(arrived[:, :, :1]), arrived[:, :, :1]], axis=2)
        halo = jnp.where(q == 0, first, arrived)
        taps12 = lax.dynamic_slice_in_dim(short_taps[1:3], half * width, width, axis=2)
        extended = jnp.concatenate([halo, blocks], axis=3).astype(jnp.float32)
        embed12 = None
        for offset in range(3):
            term = taps12[:, offset, :][:, :, None, None] * extended[
                :, :, :, 2 - offset : 2 - offset + local_tokens
            ]
            embed12 = term if embed12 is None else embed12 + term
        gate_wave = (embed12[0] * embed12[1]).astype(jnp.bfloat16)
        lanes_each = width // n_q
        outgoing12 = gate_wave.reshape(n_q, lanes_each, 2, local_tokens)
        got = lax.all_to_all(outgoing12, "cq", split_axis=0, concat_axis=0, tiled=True)
        received, got = lax.optimization_barrier((received, got))
        per_channel_view = got.transpose(1, 2, 0, 3).reshape(lanes_each, -1)
        projected0 = jnp.concatenate(list(by_half(half, own_part, received)), axis=1)
        embed0 = featured(projected0, short_taps[0:1])
        blended_lines = global_causal_smear(
            per_channel_view, spec_k, skip_gain[0], forward, inverse, tile_extent
        )
        lines, span = blended_lines.shape
        outgoing = blended_lines.reshape(lines, n_ctx, span // n_ctx).transpose(1, 0, 2)
        returned = lax.all_to_all(outgoing, ctx, split_axis=0, concat_axis=0, tiled=True)
        by_token = returned.reshape(n_ctx * lines, span // n_ctx)
        gated_output = (embed0[0] * by_token.astype(jnp.float32)).astype(jnp.bfloat16)
        return gated_output

    return shards


def solution(mesh):
    n_ctx = mesh.shape["ctx"]
    grid = np.asarray(mesh.devices).reshape(2, n_ctx // 2, mesh.shape["ch"])
    split_mesh = Mesh(grid, ("yh", "cq", "ch"))
    ctx = ("yh", "cq")
    placed = (
        P(ctx, "ch"),
        P(None, ctx, "ch"),
        P(None, None, "ch"),
        P("ch", ctx, None),
        P("ch", ctx),
    )
    mapped = jax.shard_map(
        make_shards(n_ctx, mesh.shape["ch"], BLOCK),
        mesh=split_mesh,
        in_specs=placed,
        out_specs=P("ch", ctx),
        check_vma=False,
    )
    out_sharding = NamedSharding(mesh, P("ch", "ctx"))

    def run(*args):
        return lax.with_sharding_constraint(mapped(*args), out_sharding)

    return run
```

```python
import math

import jax
import jax.numpy as jnp
from jax import lax
import numpy as np
from jax.sharding import Mesh, NamedSharding
from jax.sharding import PartitionSpec as P

BLOCK = 1024
FACTOR = 32


def shifted(block, axis, size, distance):
    route = [(i - distance, i) for i in range(size) if 0 <= i - distance < size]
    return lax.ppermute(block, axis, route)


def unit_wave(rows, cols, period, scale_rows):
    outer = rows // FACTOR
    hi = jnp.arange(outer, dtype=jnp.int32)[:, None] * (FACTOR * scale_rows)
    lo = jnp.arange(FACTOR, dtype=jnp.int32)[:, None] * scale_rows
    col = jnp.arange(cols, dtype=jnp.int32)[None, :]
    step = 2.0 * math.pi / period
    hi_phase = step * ((hi * col) % period).astype(jnp.float32)
    lo_phase = step * ((lo * col) % period).astype(jnp.float32)
    hc, hs = jnp.cos(hi_phase)[:, None, :], jnp.sin(hi_phase)[:, None, :]
    lc, ls = jnp.cos(lo_phase)[None, :, :], jnp.sin(lo_phase)[None, :, :]
    cos_t = (hc * lc - hs * ls).reshape(rows, cols)
    sin_t = (hs * lc + hc * ls).reshape(rows, cols)
    return cos_t, sin_t


def spectral_tables(tile_extent):
    period = 2 * tile_extent
    cos_f, sin_f = unit_wave(tile_extent, tile_extent, period, 1)
    alternating = jnp.where(jnp.arange(tile_extent) % 2 == 0, 1.0, -1.0).astype(jnp.float32)
    first_col = (jnp.arange(tile_extent) == 0)[None, :]
    forward = jnp.concatenate(
        [cos_f, jnp.where(first_col, alternating[:, None], -sin_f)], axis=1
    ).astype(jnp.bfloat16)
    cos_b, sin_b = unit_wave(tile_extent, period, period, 1)
    first_row = (jnp.arange(tile_extent) == 0)[:, None]
    alt_t = jnp.where(jnp.arange(period) % 2 == 0, 1.0, -1.0).astype(jnp.float32)[None, :]
    weights = jnp.where(first_row, 1.0, 2.0) / period
    inverse = jnp.concatenate(
        [weights * cos_b, jnp.where(first_row, alt_t / period, -(2.0 / period) * sin_b)], axis=0
    ).astype(jnp.bfloat16)
    return forward, inverse


def filter_spectra(kernel_table_lines, forward, tile_extent):
    lane_total, context_extent = kernel_table_lines.shape
    groups = context_extent // tile_extent
    kernel = (
        kernel_table_lines.astype(jnp.bfloat16)
        .reshape(lane_total, groups, tile_extent)
        .transpose(1, 0, 2)
        .reshape(groups * lane_total, tile_extent)
    )
    spec_k = jnp.dot(kernel, forward, preferred_element_type=jnp.float32)
    return spec_k.reshape(groups, lane_total, 2 * tile_extent)


def global_causal_smear(gate_wave, spec_k, leftover_lines, forward, inverse, tile_extent):
    lane_total, context_extent = gate_wave.shape
    groups = context_extent // tile_extent
    slot0 = (jnp.arange(tile_extent) == 0)[None, None, :]
    source = gate_wave.reshape(lane_total * groups, tile_extent)
    spec_x = jnp.dot(source, forward, preferred_element_type=jnp.float32)
    spec_x = spec_x.reshape(lane_total, groups, 2 * tile_extent)
    x_re, x_im = spec_x[:, :, :tile_extent], spec_x[:, :, tile_extent:]
    k_re, k_im = spec_k[:, :, :tile_extent], spec_k[:, :, tile_extent:]
    pad = jnp.zeros((lane_total, groups - 1, tile_extent), jnp.float32)
    xp_re = jnp.concatenate([pad, x_re], axis=1)
    xp_im = jnp.concatenate([pad, x_im], axis=1)
    rr = ii = ri = ir = None
    for offset in range(groups):
        s_re = xp_re[:, groups - 1 - offset : 2 * groups - 1 - offset]
        s_im = xp_im[:, groups - 1 - offset : 2 * groups - 1 - offset]
        f_re = k_re[offset][:, None, :]
        f_im = k_im[offset][:, None, :]
        terms = (f_re * s_re, f_im * s_im, f_re * s_im, f_im * s_re)
        if rr is None:
            rr, ii, ri, ir = terms
        else:
            rr, ii, ri, ir = rr + terms[0], ii + terms[1], ri + terms[2], ir + terms[3]
    y_re = rr - jnp.where(slot0, 0.0, ii)
    y_im = jnp.where(slot0, ii, ri + ir)
    packed = jnp.concatenate([y_re, y_im], axis=2).astype(jnp.bfloat16)
    rows = jnp.dot(
        packed.reshape(lane_total * groups, 2 * tile_extent),
        inverse,
        preferred_element_type=jnp.float32,
    ).reshape(lane_total, groups, 2 * tile_extent)
    front_half = rows[:, :, :tile_extent]
    back_half = rows[:, :, tile_extent:]
    carried = jnp.concatenate(
        [jnp.zeros((lane_total, 1, tile_extent), jnp.float32), back_half[:, :-1]], axis=1
    )
    affine_mapping = (front_half + carried).reshape(lane_total, context_extent)
    wide = gate_wave.astype(jnp.float32)
    return (affine_mapping + leftover_lines[:, None] * wide).astype(jnp.bfloat16)


def short_conv(projected_float, local_taps, previous):
    context_extent = projected_float.shape[2]
    extended = jnp.concatenate([previous, projected_float], axis=2)
    result = jnp.zeros_like(projected_float)
    for offset in range(3):
        result = (
            result
            + local_taps[:, offset, :][:, :, None]
            * extended[:, :, 2 - offset : 2 - offset + context_extent]
        )
    return result


def make_shards(n_ctx, n_ch, tile_extent):
    ctx = ("yh", "cq")
    swap = [(0, 1), (1, 0)]

    def featured(projected, taps):
        local_tokens = projected.shape[2]
        previous = shifted(projected[:, :, local_tokens - 2 :], ctx, n_ctx, 1)
        return short_conv(projected.astype(jnp.float32), taps, previous.astype(jnp.float32))

    def by_half(half, own, other):
        first = jnp.where(half == 0, own, other)
        second = jnp.where(half == 0, other, own)
        return jnp.stack([first, second])

    def shards(tokens, in_weight, short_taps, long_filter, skip_gain):
        half = lax.axis_index("yh")
        local_tokens, local_features = tokens.shape
        branches, local_rows, lanes = in_weight.shape
        width = lanes // 2
        n_q = n_ctx // 2
        own_cols = lax.dynamic_slice_in_dim(in_weight, half * width, width, axis=2)
        other_cols = lax.dynamic_slice_in_dim(in_weight, (1 - half) * width, width, axis=2)
        partner_rows = lax.ppermute(other_cols, "yh", swap)
        rows_pair = jnp.stack(list(by_half(half, own_cols, partner_rows)), axis=1)
        gathered = lax.all_gather(rows_pair, "cq", axis=2, tiled=False)
        whole_weight = gathered.reshape(branches, -1, width)
        def row_features(block):
            copies = jnp.broadcast_to(block[None], (n_ch,) + block.shape)
            pieces = lax.all_to_all(copies, "ch", split_axis=0, concat_axis=2, tiled=True)
            return pieces.reshape(local_tokens, n_ch * local_features)

        own_features = row_features(tokens)
        partner_features = row_features(lax.ppermute(tokens, "yh", swap))
        whole_tokens = jnp.concatenate(list(by_half(half, own_features, partner_features)), axis=0)
        forward, inverse = spectral_tables(tile_extent)
        spec_k = filter_spectra(long_filter[0], forward, tile_extent)
        whole_weight, forward, inverse, spec_k = lax.optimization_barrier(
            (whole_weight, forward, inverse, spec_k)
        )
        summed = jnp.einsum(
            "pdc,ld->pcl", whole_weight, whole_tokens, preferred_element_type=jnp.float32
        ).astype(jnp.bfloat16)
        own_part = lax.dynamic_slice_in_dim(summed[0:1], half * local_tokens, local_tokens, axis=2)
        other_part = lax.dynamic_slice_in_dim(
            summed[0:1], (1 - half) * local_tokens, local_tokens, axis=2
        )
        received = lax.ppermute(other_part, "yh", swap)
        q = lax.axis_index("cq")
        blocks = summed[1:3].reshape(2, width, 2, local_tokens)
        tails = blocks[:, :, :, local_tokens - 2 :].transpose(0, 2, 3, 1).reshape(-1, width)
        ring = [(i, (i + 1) % n_q) for i in range(n_q)]
        arrived = lax.ppermute(tails, "cq", ring).reshape(2, 2, 2, width).transpose(0, 3, 1, 2)
        first = jnp.concatenate([jnp.zeros_like(arrived[:, :, :1]), arrived[:, :, :1]], axis=2)
        halo = jnp.where(q == 0, first, arrived)
        taps12 = lax.dynamic_slice_in_dim(short_taps[1:3], half * width, width, axis=2)
        extended = jnp.concatenate([halo, blocks], axis=3).astype(jnp.float32)
        embed12 = None
        for offset in range(3):
            term = taps12[:, offset, :][:, :, None, None] * extended[
                :, :, :, 2 - offset : 2 - offset + local_tokens
            ]
            embed12 = term if embed12 is None else embed12 + term
        gate_wave = (embed12[0] * embed12[1]).astype(jnp.bfloat16)
        lanes_each = width // n_q
        outgoing12 = gate_wave.reshape(n_q, lanes_each, 2, local_tokens)
        got = lax.all_to_all(outgoing12, "cq", split_axis=0, concat_axis=0, tiled=True)
        received, got = lax.optimization_barrier((received, got))
        per_channel_view = got.transpose(1, 2, 0, 3).reshape(lanes_each, -1)
        projected0 = jnp.concatenate(list(by_half(half, own_part, received)), axis=1)
        embed0 = featured(projected0, short_taps[0:1])
        blended_lines = global_causal_smear(
            per_channel_view, spec_k, skip_gain[0], forward, inverse, tile_extent
        )
        lines, span = blended_lines.shape
        outgoing = blended_lines.reshape(lines, n_ctx, span // n_ctx).transpose(1, 0, 2)
        returned = lax.all_to_all(outgoing, ctx, split_axis=0, concat_axis=0, tiled=True)
        by_token = returned.reshape(n_ctx * lines, span // n_ctx)
        gated_output = (embed0[0] * by_token.astype(jnp.float32)).astype(jnp.bfloat16)
        return gated_output

    return shards


def solution(mesh):
    n_ctx = mesh.shape["ctx"]
    grid = np.asarray(mesh.devices).reshape(2, n_ctx // 2, mesh.shape["ch"])
    split_mesh = Mesh(grid, ("yh", "cq", "ch"))
    ctx = ("yh", "cq")
    placed = (
        P(ctx, "ch"),
        P(None, ctx, "ch"),
        P(None, None, "ch"),
        P("ch", ctx, None),
        P("ch", ctx),
    )
    mapped = jax.shard_map(
        make_shards(n_ctx, mesh.shape["ch"], BLOCK),
        mesh=split_mesh,
        in_specs=placed,
        out_specs=P("ch", ctx),
        check_vma=False,
    )
    out_sharding = NamedSharding(mesh, P("ch", "ctx"))

    def run(*args):
        return lax.with_sharding_constraint(mapped(*args), out_sharding)

    return run
```

```python
import math

import jax
import jax.numpy as jnp
from jax import lax
import numpy as np
from jax.sharding import Mesh, NamedSharding
from jax.sharding import PartitionSpec as P

BLOCK = 1024
FACTOR = 32
TRIPLE = lax.Precision.HIGH


def shifted(block, axis, size, distance):
    route = [(i - distance, i) for i in range(size) if 0 <= i - distance < size]
    return lax.ppermute(block, axis, route)


def unit_wave(rows, cols, period, scale_rows):
    outer = rows // FACTOR
    hi = jnp.arange(outer, dtype=jnp.int32)[:, None] * (FACTOR * scale_rows)
    lo = jnp.arange(FACTOR, dtype=jnp.int32)[:, None] * scale_rows
    col = jnp.arange(cols, dtype=jnp.int32)[None, :]
    step = 2.0 * math.pi / period
    hi_phase = step * ((hi * col) % period).astype(jnp.float32)
    lo_phase = step * ((lo * col) % period).astype(jnp.float32)
    hc, hs = jnp.cos(hi_phase)[:, None, :], jnp.sin(hi_phase)[:, None, :]
    lc, ls = jnp.cos(lo_phase)[None, :, :], jnp.sin(lo_phase)[None, :, :]
    cos_t = (hc * lc - hs * ls).reshape(rows, cols)
    sin_t = (hs * lc + hc * ls).reshape(rows, cols)
    return cos_t, sin_t


def spectral_tables(tile_extent):
    period = 2 * tile_extent
    cos_f, sin_f = unit_wave(tile_extent, tile_extent, period, 1)
    alternating = jnp.where(jnp.arange(tile_extent) % 2 == 0, 1.0, -1.0).astype(jnp.float32)
    first_col = (jnp.arange(tile_extent) == 0)[None, :]
    forward = jnp.concatenate([cos_f, jnp.where(first_col, alternating[:, None], -sin_f)], axis=1)
    cos_b, sin_b = unit_wave(tile_extent, period, period, 1)
    first_row = (jnp.arange(tile_extent) == 0)[:, None]
    alt_t = jnp.where(jnp.arange(period) % 2 == 0, 1.0, -1.0).astype(jnp.float32)[None, :]
    weights = jnp.where(first_row, 1.0, 2.0) / period
    inverse = jnp.concatenate(
        [weights * cos_b, jnp.where(first_row, alt_t / period, -(2.0 / period) * sin_b)], axis=0
    )
    return forward, inverse


def filter_spectra(kernel_table_lines, forward, tile_extent):
    lane_total, context_extent = kernel_table_lines.shape
    groups = context_extent // tile_extent
    kernel = (
        kernel_table_lines.reshape(lane_total, groups, tile_extent)
        .transpose(1, 0, 2)
        .reshape(groups * lane_total, tile_extent)
    )
    spec_k = jnp.dot(kernel, forward, precision=TRIPLE, preferred_element_type=jnp.float32)
    return spec_k.reshape(groups, lane_total, 2 * tile_extent)


def global_causal_smear(gate_wave, spec_k, leftover_lines, forward, inverse, tile_extent):
    lane_total, context_extent = gate_wave.shape
    groups = context_extent // tile_extent
    slot0 = (jnp.arange(tile_extent) == 0)[None, None, :]
    source = gate_wave.astype(jnp.float32).reshape(lane_total * groups, tile_extent)
    spec_x = jnp.dot(source, forward, precision=TRIPLE, preferred_element_type=jnp.float32)
    spec_x = spec_x.reshape(lane_total, groups, 2 * tile_extent)
    x_re, x_im = spec_x[:, :, :tile_extent], spec_x[:, :, tile_extent:]
    k_re, k_im = spec_k[:, :, :tile_extent], spec_k[:, :, tile_extent:]
    pad = jnp.zeros((lane_total, groups - 1, tile_extent), jnp.float32)
    xp_re = jnp.concatenate([pad, x_re], axis=1)
    xp_im = jnp.concatenate([pad, x_im], axis=1)
    rr = ii = ri = ir = None
    for offset in range(groups):
        s_re = xp_re[:, groups - 1 - offset : 2 * groups - 1 - offset]
        s_im = xp_im[:, groups - 1 - offset : 2 * groups - 1 - offset]
        f_re = k_re[offset][:, None, :]
        f_im = k_im[offset][:, None, :]
        terms = (f_re * s_re, f_im * s_im, f_re * s_im, f_im * s_re)
        if rr is None:
            rr, ii, ri, ir = terms
        else:
            rr, ii, ri, ir = rr + terms[0], ii + terms[1], ri + terms[2], ir + terms[3]
    y_re = rr - jnp.where(slot0, 0.0, ii)
    y_im = jnp.where(slot0, ii, ri + ir)
    packed = jnp.concatenate([y_re, y_im], axis=2)
    rows = jnp.dot(
        packed.reshape(lane_total * groups, 2 * tile_extent),
        inverse,
        precision=TRIPLE,
        preferred_element_type=jnp.float32,
    ).reshape(lane_total, groups, 2 * tile_extent)
    front_half = rows[:, :, :tile_extent]
    back_half = rows[:, :, tile_extent:]
    carried = jnp.concatenate(
        [jnp.zeros((lane_total, 1, tile_extent), jnp.float32), back_half[:, :-1]], axis=1
    )
    affine_mapping = (front_half + carried).reshape(lane_total, context_extent)
    wide = gate_wave.astype(jnp.float32)
    return (affine_mapping + leftover_lines[:, None] * wide).astype(jnp.bfloat16)


def short_conv(projected_float, local_taps, previous):
    context_extent = projected_float.shape[2]
    extended = jnp.concatenate([previous, projected_float], axis=2)
    result = jnp.zeros_like(projected_float)
    for offset in range(3):
        result = (
            result
            + local_taps[:, offset, :][:, :, None]
            * extended[:, :, 2 - offset : 2 - offset + context_extent]
        )
    return result


def make_shards(n_ctx, n_ch, tile_extent):
    ctx = ("yh", "cq")
    swap = [(0, 1), (1, 0)]

    def featured(projected, taps):
        local_tokens = projected.shape[2]
        previous = shifted(projected[:, :, local_tokens - 2 :], ctx, n_ctx, 1)
        return short_conv(projected.astype(jnp.float32), taps, previous.astype(jnp.float32))

    def by_half(half, own, other):
        first = jnp.where(half == 0, own, other)
        second = jnp.where(half == 0, other, own)
        return jnp.stack([first, second])

    def shards(tokens, in_weight, short_taps, long_filter, skip_gain):
        half = lax.axis_index("yh")
        local_tokens, local_features = tokens.shape
        branches, local_rows, lanes = in_weight.shape
        width = lanes // 2
        n_q = n_ctx // 2
        own_cols = lax.dynamic_slice_in_dim(in_weight, half * width, width, axis=2)
        other_cols = lax.dynamic_slice_in_dim(in_weight, (1 - half) * width, width, axis=2)
        partner_rows = lax.ppermute(other_cols, "yh", swap)
        rows_pair = jnp.stack(list(by_half(half, own_cols, partner_rows)), axis=1)
        gathered = lax.all_gather(rows_pair, "cq", axis=2, tiled=False)
        whole_weight = gathered.reshape(branches, -1, width)
        def row_features(block):
            copies = jnp.broadcast_to(block[None], (n_ch,) + block.shape)
            pieces = lax.all_to_all(copies, "ch", split_axis=0, concat_axis=2, tiled=True)
            return pieces.reshape(local_tokens, n_ch * local_features)

        own_features = row_features(tokens)
        partner_features = row_features(lax.ppermute(tokens, "yh", swap))
        whole_tokens = jnp.concatenate(list(by_half(half, own_features, partner_features)), axis=0)
        forward, inverse = spectral_tables(tile_extent)
        spec_k = filter_spectra(long_filter[0], forward, tile_extent)
        whole_weight, forward, inverse, spec_k = lax.optimization_barrier(
            (whole_weight, forward, inverse, spec_k)
        )
        summed = jnp.einsum(
            "pdc,ld->pcl", whole_weight, whole_tokens, preferred_element_type=jnp.float32
        ).astype(jnp.bfloat16)
        own_part = lax.dynamic_slice_in_dim(summed[0:1], half * local_tokens, local_tokens, axis=2)
        other_part = lax.dynamic_slice_in_dim(
            summed[0:1], (1 - half) * local_tokens, local_tokens, axis=2
        )
        received = lax.ppermute(other_part, "yh", swap)
        q = lax.axis_index("cq")
        blocks = summed[1:3].reshape(2, width, 2, local_tokens)
        tails = blocks[:, :, :, local_tokens - 2 :].transpose(0, 2, 3, 1).reshape(-1, width)
        ring = [(i, (i + 1) % n_q) for i in range(n_q)]
        arrived = lax.ppermute(tails, "cq", ring).reshape(2, 2, 2, width).transpose(0, 3, 1, 2)
        first = jnp.concatenate([jnp.zeros_like(arrived[:, :, :1]), arrived[:, :, :1]], axis=2)
        halo = jnp.where(q == 0, first, arrived)
        taps12 = lax.dynamic_slice_in_dim(short_taps[1:3], half * width, width, axis=2)
        extended = jnp.concatenate([halo, blocks], axis=3).astype(jnp.float32)
        embed12 = None
        for offset in range(3):
            term = taps12[:, offset, :][:, :, None, None] * extended[
                :, :, :, 2 - offset : 2 - offset + local_tokens
            ]
            embed12 = term if embed12 is None else embed12 + term
        gate_wave = (embed12[0] * embed12[1]).astype(jnp.bfloat16)
        lanes_each = width // n_q
        outgoing12 = gate_wave.reshape(n_q, lanes_each, 2, local_tokens)
        got = lax.all_to_all(outgoing12, "cq", split_axis=0, concat_axis=0, tiled=True)
        received, got = lax.optimization_barrier((received, got))
        per_channel_view = got.transpose(1, 2, 0, 3).reshape(lanes_each, -1)
        projected0 = jnp.concatenate(list(by_half(half, own_part, received)), axis=1)
        embed0 = featured(projected0, short_taps[0:1])
        blended_lines = global_causal_smear(
            per_channel_view, spec_k, skip_gain[0], forward, inverse, tile_extent
        )
        lines, span = blended_lines.shape
        outgoing = blended_lines.reshape(lines, n_ctx, span // n_ctx).transpose(1, 0, 2)
        returned = lax.all_to_all(outgoing, ctx, split_axis=0, concat_axis=0, tiled=True)
        by_token = returned.reshape(n_ctx * lines, span // n_ctx)
        gated_output = (embed0[0] * by_token.astype(jnp.float32)).astype(jnp.bfloat16)
        return gated_output

    return shards


def solution(mesh):
    n_ctx = mesh.shape["ctx"]
    grid = np.asarray(mesh.devices).reshape(2, n_ctx // 2, mesh.shape["ch"])
    split_mesh = Mesh(grid, ("yh", "cq", "ch"))
    ctx = ("yh", "cq")
    placed = (
        P(ctx, "ch"),
        P(None, ctx, "ch"),
        P(None, None, "ch"),
        P("ch", ctx, None),
        P("ch", ctx),
    )
    mapped = jax.shard_map(
        make_shards(n_ctx, mesh.shape["ch"], BLOCK),
        mesh=split_mesh,
        in_specs=placed,
        out_specs=P("ch", ctx),
        check_vma=False,
    )
    out_sharding = NamedSharding(mesh, P("ch", "ctx"))

    def run(*args):
        return lax.with_sharding_constraint(mapped(*args), out_sharding)

    return run
```

```python
import math

import jax
import jax.numpy as jnp
from jax import lax
import numpy as np
from jax.sharding import Mesh, NamedSharding
from jax.sharding import PartitionSpec as P

BLOCK = 1024
FACTOR = 32
TRIPLE = lax.Precision.HIGH


def shifted(block, axis, size, distance):
    route = [(i - distance, i) for i in range(size) if 0 <= i - distance < size]
    return lax.ppermute(block, axis, route)


def unit_wave(rows, cols, period, scale_rows):
    outer = rows // FACTOR
    hi = jnp.arange(outer, dtype=jnp.int32)[:, None] * (FACTOR * scale_rows)
    lo = jnp.arange(FACTOR, dtype=jnp.int32)[:, None] * scale_rows
    col = jnp.arange(cols, dtype=jnp.int32)[None, :]
    step = 2.0 * math.pi / period
    hi_phase = step * ((hi * col) % period).astype(jnp.float32)
    lo_phase = step * ((lo * col) % period).astype(jnp.float32)
    hc, hs = jnp.cos(hi_phase)[:, None, :], jnp.sin(hi_phase)[:, None, :]
    lc, ls = jnp.cos(lo_phase)[None, :, :], jnp.sin(lo_phase)[None, :, :]
    cos_t = (hc * lc - hs * ls).reshape(rows, cols)
    sin_t = (hs * lc + hc * ls).reshape(rows, cols)
    return cos_t, sin_t


def spectral_tables(tile_extent):
    period = 2 * tile_extent
    cos_f, sin_f = unit_wave(tile_extent, tile_extent, period, 1)
    alternating = jnp.where(jnp.arange(tile_extent) % 2 == 0, 1.0, -1.0).astype(jnp.float32)
    first_col = (jnp.arange(tile_extent) == 0)[None, :]
    forward = jnp.concatenate([cos_f, jnp.where(first_col, alternating[:, None], -sin_f)], axis=1)
    cos_b, sin_b = unit_wave(tile_extent, period, period, 1)
    first_row = (jnp.arange(tile_extent) == 0)[:, None]
    alt_t = jnp.where(jnp.arange(period) % 2 == 0, 1.0, -1.0).astype(jnp.float32)[None, :]
    weights = jnp.where(first_row, 1.0, 2.0) / period
    inverse = jnp.concatenate(
        [weights * cos_b, jnp.where(first_row, alt_t / period, -(2.0 / period) * sin_b)], axis=0
    )
    return forward, inverse


def filter_spectra(kernel_table_lines, forward, tile_extent):
    lane_total, context_extent = kernel_table_lines.shape
    groups = context_extent // tile_extent
    kernel = (
        kernel_table_lines.reshape(lane_total, groups, tile_extent)
        .transpose(1, 0, 2)
        .reshape(groups * lane_total, tile_extent)
    )
    spec_k = jnp.dot(kernel, forward, precision=TRIPLE, preferred_element_type=jnp.float32)
    return spec_k.reshape(groups, lane_total, 2 * tile_extent)


def global_causal_smear(gate_wave, spec_k, leftover_lines, forward, inverse, tile_extent):
    lane_total, context_extent = gate_wave.shape
    groups = context_extent // tile_extent
    slot0 = (jnp.arange(tile_extent) == 0)[None, None, :]
    source = gate_wave.reshape(lane_total * groups, tile_extent)
    forward_hi = forward.astype(jnp.bfloat16)
    forward_lo = (forward - forward_hi.astype(jnp.float32)).astype(jnp.bfloat16)
    spec_x = jnp.dot(source, forward_hi, preferred_element_type=jnp.float32) + jnp.dot(
        source, forward_lo, preferred_element_type=jnp.float32
    )
    spec_x = spec_x.reshape(lane_total, groups, 2 * tile_extent)
    x_re, x_im = spec_x[:, :, :tile_extent], spec_x[:, :, tile_extent:]
    k_re, k_im = spec_k[:, :, :tile_extent], spec_k[:, :, tile_extent:]
    pad = jnp.zeros((lane_total, groups - 1, tile_extent), jnp.float32)
    xp_re = jnp.concatenate([pad, x_re], axis=1)
    xp_im = jnp.concatenate([pad, x_im], axis=1)
    rr = ii = ri = ir = None
    for offset in range(groups):
        s_re = xp_re[:, groups - 1 - offset : 2 * groups - 1 - offset]
        s_im = xp_im[:, groups - 1 - offset : 2 * groups - 1 - offset]
        f_re = k_re[offset][:, None, :]
        f_im = k_im[offset][:, None, :]
        terms = (f_re * s_re, f_im * s_im, f_re * s_im, f_im * s_re)
        if rr is None:
            rr, ii, ri, ir = terms
        else:
            rr, ii, ri, ir = rr + terms[0], ii + terms[1], ri + terms[2], ir + terms[3]
    y_re = rr - jnp.where(slot0, 0.0, ii)
    y_im = jnp.where(slot0, ii, ri + ir)
    packed = jnp.concatenate([y_re, y_im], axis=2)
    rows = jnp.dot(
        packed.reshape(lane_total * groups, 2 * tile_extent),
        inverse,
        precision=TRIPLE,
        preferred_element_type=jnp.float32,
    ).reshape(lane_total, groups, 2 * tile_extent)
    front_half = rows[:, :, :tile_extent]
    back_half = rows[:, :, tile_extent:]
    carried = jnp.concatenate(
        [jnp.zeros((lane_total, 1, tile_extent), jnp.float32), back_half[:, :-1]], axis=1
    )
    affine_mapping = (front_half + carried).reshape(lane_total, context_extent)
    wide = gate_wave.astype(jnp.float32)
    return (affine_mapping + leftover_lines[:, None] * wide).astype(jnp.bfloat16)


def short_conv(projected_float, local_taps, previous):
    context_extent = projected_float.shape[2]
    extended = jnp.concatenate([previous, projected_float], axis=2)
    result = jnp.zeros_like(projected_float)
    for offset in range(3):
        result = (
            result
            + local_taps[:, offset, :][:, :, None]
            * extended[:, :, 2 - offset : 2 - offset + context_extent]
        )
    return result


def make_shards(n_ctx, n_ch, tile_extent):
    ctx = ("yh", "cq")
    swap = [(0, 1), (1, 0)]

    def featured(projected, taps):
        local_tokens = projected.shape[2]
        previous = shifted(projected[:, :, local_tokens - 2 :], ctx, n_ctx, 1)
        return short_conv(projected.astype(jnp.float32), taps, previous.astype(jnp.float32))

    def by_half(half, own, other):
        first = jnp.where(half == 0, own, other)
        second = jnp.where(half == 0, other, own)
        return jnp.stack([first, second])

    def shards(tokens, in_weight, short_taps, long_filter, skip_gain):
        half = lax.axis_index("yh")
        local_tokens, local_features = tokens.shape
        branches, local_rows, lanes = in_weight.shape
        width = lanes // 2
        n_q = n_ctx // 2
        own_cols = lax.dynamic_slice_in_dim(in_weight, half * width, width, axis=2)
        other_cols = lax.dynamic_slice_in_dim(in_weight, (1 - half) * width, width, axis=2)
        partner_rows = lax.ppermute(other_cols, "yh", swap)
        rows_pair = jnp.stack(list(by_half(half, own_cols, partner_rows)), axis=1)
        gathered = lax.all_gather(rows_pair, "cq", axis=2, tiled=False)
        whole_weight = gathered.reshape(branches, -1, width)
        def row_features(block):
            copies = jnp.broadcast_to(block[None], (n_ch,) + block.shape)
            pieces = lax.all_to_all(copies, "ch", split_axis=0, concat_axis=2, tiled=True)
            return pieces.reshape(local_tokens, n_ch * local_features)

        own_features = row_features(tokens)
        partner_features = row_features(lax.ppermute(tokens, "yh", swap))
        whole_tokens = jnp.concatenate(list(by_half(half, own_features, partner_features)), axis=0)
        forward, inverse = spectral_tables(tile_extent)
        spec_k = filter_spectra(long_filter[0], forward, tile_extent)
        whole_weight, forward, inverse, spec_k = lax.optimization_barrier(
            (whole_weight, forward, inverse, spec_k)
        )
        summed = jnp.einsum(
            "pdc,ld->pcl", whole_weight, whole_tokens, preferred_element_type=jnp.float32
        ).astype(jnp.bfloat16)
        own_part = lax.dynamic_slice_in_dim(summed[0:1], half * local_tokens, local_tokens, axis=2)
        other_part = lax.dynamic_slice_in_dim(
            summed[0:1], (1 - half) * local_tokens, local_tokens, axis=2
        )
        received = lax.ppermute(other_part, "yh", swap)
        q = lax.axis_index("cq")
        blocks = summed[1:3].reshape(2, width, 2, local_tokens)
        tails = blocks[:, :, :, local_tokens - 2 :].transpose(0, 2, 3, 1).reshape(-1, width)
        ring = [(i, (i + 1) % n_q) for i in range(n_q)]
        arrived = lax.ppermute(tails, "cq", ring).reshape(2, 2, 2, width).transpose(0, 3, 1, 2)
        first = jnp.concatenate([jnp.zeros_like(arrived[:, :, :1]), arrived[:, :, :1]], axis=2)
        halo = jnp.where(q == 0, first, arrived)
        taps12 = lax.dynamic_slice_in_dim(short_taps[1:3], half * width, width, axis=2)
        extended = jnp.concatenate([halo, blocks], axis=3).astype(jnp.float32)
        embed12 = None
        for offset in range(3):
            term = taps12[:, offset, :][:, :, None, None] * extended[
                :, :, :, 2 - offset : 2 - offset + local_tokens
            ]
            embed12 = term if embed12 is None else embed12 + term
        gate_wave = (embed12[0] * embed12[1]).astype(jnp.bfloat16)
        lanes_each = width // n_q
        outgoing12 = gate_wave.reshape(n_q, lanes_each, 2, local_tokens)
        got = lax.all_to_all(outgoing12, "cq", split_axis=0, concat_axis=0, tiled=True)
        received, got = lax.optimization_barrier((received, got))
        per_channel_view = got.transpose(1, 2, 0, 3).reshape(lanes_each, -1)
        projected0 = jnp.concatenate(list(by_half(half, own_part, received)), axis=1)
        embed0 = featured(projected0, short_taps[0:1])
        blended_lines = global_causal_smear(
            per_channel_view, spec_k, skip_gain[0], forward, inverse, tile_extent
        )
        lines, span = blended_lines.shape
        outgoing = blended_lines.reshape(lines, n_ctx, span // n_ctx).transpose(1, 0, 2)
        returned = lax.all_to_all(outgoing, ctx, split_axis=0, concat_axis=0, tiled=True)
        by_token = returned.reshape(n_ctx * lines, span // n_ctx)
        gated_output = (embed0[0] * by_token.astype(jnp.float32)).astype(jnp.bfloat16)
        return gated_output

    return shards


def solution(mesh):
    n_ctx = mesh.shape["ctx"]
    grid = np.asarray(mesh.devices).reshape(2, n_ctx // 2, mesh.shape["ch"])
    split_mesh = Mesh(grid, ("yh", "cq", "ch"))
    ctx = ("yh", "cq")
    placed = (
        P(ctx, "ch"),
        P(None, ctx, "ch"),
        P(None, None, "ch"),
        P("ch", ctx, None),
        P("ch", ctx),
    )
    mapped = jax.shard_map(
        make_shards(n_ctx, mesh.shape["ch"], BLOCK),
        mesh=split_mesh,
        in_specs=placed,
        out_specs=P("ch", ctx),
        check_vma=False,
    )
    out_sharding = NamedSharding(mesh, P("ch", "ctx"))

    def run(*args):
        return lax.with_sharding_constraint(mapped(*args), out_sharding)

    return run
```
